32 devices in a mesh: row: 4 (over y, core), col: 8 (over z, x).
Axes of the slice: x: 2, y: 2, z: 4, core: 2. Of those that a mesh axis runs over, the one named last changes fastest.
Arguments:
- tokens: bfloat16 [512, 16384], P('col', 'row'), may hold values from -6 to 6
- gate_packed: bfloat16 [2560, 1024, 128], P('row', 'col'), may hold values from -0.0625 to 0.0625
- up_packed: bfloat16 [2560, 1024, 128], P('row', 'col'), may hold values from -0.0625 to 0.0625
- down_packed: bfloat16 [5120, 512, 128], P('col', 'row'), may hold values from -0.0546875 to 0.0546875
- gate_keep: int32 [128, 208], P('row', 'col'), may hold values from 0 to 1, as said below
- down_keep: int32 [208, 128], P('col', 'row'), may hold values from 0 to 1, as said below
Outputs:
- mixed: bfloat16 [512, 16384], P('col', 'row')
The draws below stay inside these ranges and needn't reach their ends.
Inputs may be any that keep to these rules, and one draw needn't show every extreme that they name: `gate_keep`: in every tile of 32 x 26 blocks, at least 160 and at most 640 blocks are kept; some tile keeps exactly 640. `down_keep`: in every tile of 26 x 32 blocks, at least 160 and at most 640 blocks are kept; some tile keeps exactly 640.
All inputs are finite; a program needn't handle non-finite values.
Results may differ from the reference program's by a relative error of at most 0.02.
Values may be sent and summed in bfloat16 or wider, within the bound.
No kernel may reach another device: no remote copies, remote signals or barrier semaphores. Data moves between devices by JAX's collectives and lax.ppermute only.
A program may use at most 320 MiB of HBM per device.

```python
import jax
import jax.numpy as jnp
from jax import lax

D = 16384
FF = 26624
BS = 128
TOKENS = 512
DBLK = 32
FBLK = 26
CAP = 640
N_ROW = 4
N_COL = 8


def tile_masks(key, tile_count, block_count, capacity):
    first, second, third = jax.random.split(key, 3)
    counts = jax.random.randint(first, (tile_count,), capacity // 4, capacity + 1)
    fullest = jax.random.randint(second, (), 0, tile_count)
    counts = jnp.where(jnp.arange(tile_count) == fullest, capacity, counts)
    tile_keys = jax.random.split(third, tile_count)
    orders = jax.vmap(lambda tile_key: jax.random.permutation(tile_key, block_count))(tile_keys)
    return (orders < counts[:, None]).astype(jnp.int32)


def draw_gate_keep(key, part):
    masks = tile_masks(jax.random.fold_in(key, 11), N_ROW * N_COL, DBLK * FBLK, CAP)
    masks = masks.reshape(N_ROW, N_COL, DBLK, FBLK).transpose(0, 2, 1, 3)
    return masks.reshape(N_ROW * DBLK, N_COL * FBLK)


def draw_down_keep(key, part):
    masks = tile_masks(jax.random.fold_in(key, 23), N_COL * N_ROW, FBLK * DBLK, CAP)
    masks = masks.reshape(N_COL, N_ROW, FBLK, DBLK).transpose(0, 2, 1, 3)
    return masks.reshape(N_COL * FBLK, N_ROW * DBLK)


def shard_levels(stream_key, shape, cuts, smallest, top_value):
    factor_of = 1.0
    for axis_at, shards_of in cuts:
        heights = jax.random.uniform(jax.random.fold_in(jax.random.fold_in(stream_key, 6), axis_at), (shards_of,), jnp.float32, smallest / len(cuts), top_value / len(cuts))
        factor_of = factor_of * jnp.repeat(jnp.exp(heights), shape[axis_at] // shards_of).reshape((-1,) + (1,) * (len(shape) - 1 - axis_at))
    return factor_of


def gaussian(stream_key, dims, spread, most, pieces=(), held_as=jnp.bfloat16):
    level = shard_levels(stream_key, dims, pieces, -0.22, 0.18) if pieces else 1.0
    values = jax.random.normal(stream_key, dims, jnp.float32) * spread * level
    return jnp.minimum(jnp.maximum(values, -most), most).astype(held_as)


def setup_inputs(seed: int = 0) -> dict:
    keys = jax.random.split(jax.random.key(seed), 7)
    return {
        "tokens": gaussian(keys[0], (TOKENS, D), 1.0, 6.0, ((0, 8), (1, 4))),
        "gate_packed": gaussian(keys[1], (N_ROW * CAP, N_COL * BS, BS), (D // 2) ** -0.5, 0.0625, ((0, 4), (1, 8))),
        "up_packed": gaussian(keys[2], (N_ROW * CAP, N_COL * BS, BS), (D // 2) ** -0.5, 0.0625, ((0, 4), (1, 8))),
        "down_packed": gaussian(keys[3], (N_COL * CAP, N_ROW * BS, BS), (FF // 2) ** -0.5, 0.0546875, ((0, 8), (1, 4))),
        "gate_keep": draw_gate_keep(jax.random.fold_in(keys[6], 71), 0),
        "down_keep": draw_down_keep(jax.random.fold_in(keys[6], 71), 0),
    }


def dense_slab(packed_slab, keep_slab, n_inner, in_blocks, out_blocks):
    capacity = packed_slab.shape[0]
    block = packed_slab.shape[2]
    tiles = packed_slab.reshape(capacity, n_inner, block, block).transpose(1, 0, 2, 3)
    masks = keep_slab.reshape(in_blocks, n_inner, out_blocks).transpose(1, 0, 2).reshape(n_inner, in_blocks * out_blocks)

    def one_tile(tile_blocks, mask_flat):
        position = (jnp.cumsum(mask_flat) - 1).astype(jnp.int32)
        slot_index = jnp.where(mask_flat == 1, position, 0).astype(jnp.int32)
        picked = tile_blocks[slot_index] * mask_flat.astype(packed_slab.dtype)[:, None, None]
        return picked.reshape(in_blocks, out_blocks, block, block)

    blocks = jax.vmap(one_tile)(tiles, masks)
    return blocks.transpose(1, 3, 0, 2, 4).reshape(in_blocks * block, n_inner * out_blocks * block)


def reference(tokens, gate_packed, up_packed, down_packed, gate_keep, down_keep):
    row_width = DBLK * BS
    col_width = FBLK * BS
    gate_sum = jnp.zeros((TOKENS, FF), jnp.float32)
    up_sum = jnp.zeros((TOKENS, FF), jnp.float32)
    for i in range(N_ROW):
        panel = tokens[:, i * row_width:(i + 1) * row_width].astype(jnp.float32)
        keep_slab = gate_keep[i * DBLK:(i + 1) * DBLK]
        gate_dense = dense_slab(gate_packed[i * CAP:(i + 1) * CAP], keep_slab, N_COL, DBLK, FBLK)
        up_dense = dense_slab(up_packed[i * CAP:(i + 1) * CAP], keep_slab, N_COL, DBLK, FBLK)
        gate_part = jnp.dot(panel, gate_dense.astype(jnp.float32)).astype(jnp.bfloat16)
        up_part = jnp.dot(panel, up_dense.astype(jnp.float32)).astype(jnp.bfloat16)
        gate_part, up_part = lax.optimization_barrier((gate_part, up_part))
        gate_sum = gate_sum + gate_part.astype(jnp.float32)
        up_sum = up_sum + up_part.astype(jnp.float32)
    hidden = (jax.nn.silu(gate_sum) * up_sum).astype(jnp.bfloat16)
    mixed = jnp.zeros((TOKENS, D), jnp.float32)
    for j in range(N_COL):
        down_dense = dense_slab(down_packed[j * CAP:(j + 1) * CAP], down_keep[j * FBLK:(j + 1) * FBLK], N_ROW, FBLK, DBLK)
        segment = hidden[:, j * col_width:(j + 1) * col_width].astype(jnp.float32)
        mixed = mixed + jnp.dot(segment, down_dense.astype(jnp.float32))
    return mixed.astype(jnp.bfloat16)
```

```python
import functools

import jax
import jax.numpy as jnp
from jax import lax
from jax.experimental import pallas as pl
from jax.experimental.pallas import tpu as pltpu
from jax.sharding import PartitionSpec as P


def slot_tables(keep, cap):
    rows, cols = keep.shape
    flat = keep.reshape(-1).astype(jnp.int32)
    slot = (jnp.cumsum(flat) - flat).reshape(rows, cols)
    base = jnp.minimum(slot[:, 0], cap - cols)
    index = jnp.where(keep == 1, slot - base[:, None], -1)
    return base.astype(jnp.int32), index.reshape(-1).astype(jnp.int32)


def sparse_kernel(base_ref, index_ref, x_ref, *refs, n_w, cols, block):
    w_refs = refs[:n_w]
    o_refs = refs[n_w:2 * n_w]
    acc_refs = refs[2 * n_w:]
    r = pl.program_id(0)

    @pl.when(r == 0)
    def _():
        for acc in acc_refs:
            acc[...] = jnp.zeros(acc.shape, acc.dtype)

    for c in range(cols):
        k = index_ref[r * cols + c]

        @pl.when(k >= 0)
        def _():
            x = x_ref[...]
            for w, acc in zip(w_refs, acc_refs):
                acc[c] += jnp.dot(x, w[k], preferred_element_type=jnp.float32)

    @pl.when(r == pl.num_programs(0) - 1)
    def _():
        for o, acc in zip(o_refs, acc_refs):
            for c in range(cols):
                o[:, c * block:(c + 1) * block] = acc[c].astype(o.dtype)


def sparse_matmul(x, packed, keep):
    rows, cols = keep.shape
    cap, block, _ = packed[0].shape
    t = x.shape[0]
    n_w = len(packed)
    base, index = slot_tables(keep, cap)
    w_spec = pl.BlockSpec((pl.Element(cols), pl.Element(block), pl.Element(block)), lambda r, b, i: (b[r], 0, 0))
    kernel = functools.partial(sparse_kernel, n_w=n_w, cols=cols, block=block)
    flops = 2 * t * block * block * rows * cols * n_w
    bytes_accessed = x.size * 2 + n_w * (cap * block * block * 2 + t * cols * block * 2)
    return pl.pallas_call(
        kernel,
        grid_spec=pltpu.PrefetchScalarGridSpec(
            num_scalar_prefetch=2,
            grid=(rows,),
            in_specs=[pl.BlockSpec((t, block), lambda r, b, i: (0, r))] + [w_spec] * n_w,
            out_specs=[pl.BlockSpec((t, cols * block), lambda r, b, i: (0, 0))] * n_w,
            scratch_shapes=[pltpu.VMEM((cols, t, block), jnp.float32)] * n_w,
        ),
        out_shape=[jax.ShapeDtypeStruct((t, cols * block), jnp.bfloat16)] * n_w,
        compiler_params=pltpu.CompilerParams(dimension_semantics=("arbitrary",)),
        cost_estimate=pl.CostEstimate(flops=flops, transcendentals=0, bytes_accessed=bytes_accessed),
    )(base, index, x, *packed)


def local(tokens, gate_packed, up_packed, down_packed, gate_keep, down_keep):
    segment = lax.all_gather(tokens, "col", axis=0, tiled=True)
    gate_rows, up_rows = sparse_matmul(segment, [gate_packed, up_packed], gate_keep)
    gate_sum, up_sum = (
        lax.psum(gate_rows, "row").astype(jnp.float32),
        lax.psum(up_rows, "row").astype(jnp.float32),
    )
    every_hidden = (jax.nn.silu(gate_sum) * up_sum).astype(jnp.bfloat16)
    (partial_out,) = sparse_matmul(every_hidden, [down_packed], down_keep)
    summed = lax.psum_scatter(partial_out, "col", scatter_dimension=0, tiled=True)
    return summed


def solution(mesh):
    in_specs = (
        P("col", "row"),
        P("row", "col", None),
        P("row", "col", None),
        P("col", "row", None),
        P("row", "col"),
        P("col", "row"),
    )
    out_specs = P("col", "row")
    return jax.shard_map(local, mesh=mesh, in_specs=in_specs, out_specs=out_specs, check_vma=False)
```

```python
import functools

import jax
import jax.numpy as jnp
from jax import lax
from jax.experimental import pallas as pl
from jax.experimental.pallas import tpu as pltpu
from jax.sharding import PartitionSpec as P


def slot_tables(keep, cap):
    rows, cols = keep.shape
    flat = keep.reshape(-1).astype(jnp.int32)
    slot = (jnp.cumsum(flat) - flat).reshape(rows, cols)
    base = jnp.minimum(slot[:, 0], cap - cols)
    index = jnp.where(keep == 1, slot - base[:, None], -1)
    return base.astype(jnp.int32), index.reshape(-1).astype(jnp.int32)


def sparse_kernel(base_ref, index_ref, x_ref, *refs, n_w, cols, block):
    w_refs = refs[:n_w]
    o_refs = refs[n_w:2 * n_w]
    acc_refs = refs[2 * n_w:]
    r = pl.program_id(0)

    @pl.when(r == 0)
    def _():
        for acc in acc_refs:
            acc[...] = jnp.zeros(acc.shape, acc.dtype)

    for c in range(cols):
        k = index_ref[r * cols + c]

        @pl.when(k >= 0)
        def _():
            x = x_ref[...]
            for w, acc in zip(w_refs, acc_refs):
                acc[c] += jnp.dot(x, w[k], preferred_element_type=jnp.float32)

    @pl.when(r == pl.num_programs(0) - 1)
    def _():
        for o, acc in zip(o_refs, acc_refs):
            for c in range(cols):
                o[:, c * block:(c + 1) * block] = acc[c].astype(o.dtype)


def sparse_matmul(x, packed, keep):
    rows, cols = keep.shape
    cap, block, _ = packed[0].shape
    t = x.shape[0]
    n_w = len(packed)
    base, index = slot_tables(keep, cap)
    w_spec = pl.BlockSpec((pl.Element(cols), pl.Element(block), pl.Element(block)), lambda r, b, i: (b[r], 0, 0))
    kernel = functools.partial(sparse_kernel, n_w=n_w, cols=cols, block=block)
    flops = 2 * t * block * block * rows * cols * n_w
    bytes_accessed = x.size * 2 + n_w * (cap * block * block * 2 + t * cols * block * 2)
    return pl.pallas_call(
        kernel,
        grid_spec=pltpu.PrefetchScalarGridSpec(
            num_scalar_prefetch=2,
            grid=(rows,),
            in_specs=[pl.BlockSpec((t, block), lambda r, b, i: (0, r))] + [w_spec] * n_w,
            out_specs=[pl.BlockSpec((t, cols * block), lambda r, b, i: (0, 0))] * n_w,
            scratch_shapes=[pltpu.VMEM((cols, t, block), jnp.float32)] * n_w,
        ),
        out_shape=[jax.ShapeDtypeStruct((t, cols * block), jnp.bfloat16)] * n_w,
        compiler_params=pltpu.CompilerParams(dimension_semantics=("arbitrary",)),
        cost_estimate=pl.CostEstimate(flops=flops, transcendentals=0, bytes_accessed=bytes_accessed),
    )(base, index, x, *packed)


def exchange(x, axis, n, bit):
    pairs = [(i, i ^ (1 << bit)) for i in range(n)]
    return lax.ppermute(x, axis, perm=pairs)


def halving_scatter(parts, axis, n, bits):
    me = lax.axis_index(axis)
    for bit in bits:
        half = parts[0].shape[0] // 2
        mine = (me >> bit) & 1
        keep = [lax.dynamic_slice_in_dim(p, mine * half, half, axis=0) for p in parts]
        send = [lax.dynamic_slice_in_dim(p, (1 - mine) * half, half, axis=0) for p in parts]
        got = exchange(tuple(s.astype(jnp.bfloat16) for s in send), axis, n, bit)
        parts = [k.astype(jnp.float32) + g.astype(jnp.float32) for k, g in zip(keep, got)]
    return parts


def doubling_gather(x, axis, n, bits):
    me = lax.axis_index(axis)
    for bit in bits:
        got = exchange(x, axis, n, bit)
        low = ((me >> bit) & 1) == 0
        x = jnp.where(low, jnp.concatenate([x, got], 0), jnp.concatenate([got, x], 0))
    return x


def local(tokens, gate_packed, up_packed, down_packed, gate_keep, down_keep):
    n_row = lax.axis_size("row")
    n_col = lax.axis_size("col")
    row_bits = list(range(n_row.bit_length() - 1))
    col_bits = list(range(n_col.bit_length() - 1))
    segment = doubling_gather(tokens, "col", n_col, col_bits[::-1])
    gate_rows, up_rows = sparse_matmul(segment, [gate_packed, up_packed], gate_keep)
    gate_sum, up_sum = halving_scatter([gate_rows, up_rows], "row", n_row, row_bits)
    hidden_share = (jax.nn.silu(gate_sum) * up_sum).astype(jnp.bfloat16)
    every_hidden = doubling_gather(hidden_share, "row", n_row, row_bits[::-1])
    (partial_out,) = sparse_matmul(every_hidden, [down_packed], down_keep)
    (summed,) = halving_scatter([partial_out], "col", n_col, col_bits)
    return summed.astype(jnp.bfloat16)


def solution(mesh):
    in_specs = (
        P("col", "row"),
        P("row", "col", None),
        P("row", "col", None),
        P("col", "row", None),
        P("row", "col"),
        P("col", "row"),
    )
    out_specs = P("col", "row")
    return jax.shard_map(local, mesh=mesh, in_specs=in_specs, out_specs=out_specs, check_vma=False)
```

```python
import functools

import jax
import jax.numpy as jnp
from jax import lax
from jax.experimental import pallas as pl
from jax.experimental.pallas import tpu as pltpu
from jax.sharding import PartitionSpec as P


def slot_tables(keep, cap):
    rows, cols = keep.shape
    flat = keep.reshape(-1).astype(jnp.int32)
    slot = (jnp.cumsum(flat) - flat).reshape(rows, cols)
    base = jnp.minimum(slot[:, 0], cap - cols)
    index = jnp.where(keep == 1, slot - base[:, None], -1)
    return base.astype(jnp.int32), index.reshape(-1).astype(jnp.int32)


def sparse_kernel(base_ref, index_ref, x_ref, *refs, n_w, group, cols, block):
    w_refs = refs[:n_w * group]
    o_refs = refs[n_w * group:n_w * group + n_w]
    acc_refs = refs[n_w * group + n_w:n_w * group + 2 * n_w]
    panel_refs = refs[n_w * group + 2 * n_w:]
    g = pl.program_id(0)

    @pl.when(g == 0)
    def _():
        for acc in acc_refs:
            acc[...] = jnp.zeros(acc.shape, acc.dtype)

    for rr in range(group):
        for c in range(cols):
            k = index_ref[(g * group + rr) * cols + c]
            for a in range(n_w):
                blk = w_refs[a * group + rr][jnp.maximum(k, 0)]
                panel_refs[a][rr * block:(rr + 1) * block, c * block:(c + 1) * block] = jnp.where(
                    k >= 0, blk, jnp.zeros_like(blk))

    x = x_ref[...]
    for panel, acc in zip(panel_refs, acc_refs):
        acc[...] += jnp.dot(x, panel[...], preferred_element_type=jnp.float32)

    @pl.when(g == pl.num_programs(0) - 1)
    def _():
        for o, acc in zip(o_refs, acc_refs):
            o[...] = acc[...].astype(o.dtype)


def sparse_matmul(x, packed, keep):
    rows, cols = keep.shape
    cap, block, _ = packed[0].shape
    t = x.shape[0]
    n_w = len(packed)
    group = next(s for s in (4, 2, 1) if rows % s == 0)
    base, index = slot_tables(keep, cap)

    def w_spec(rr):
        return pl.BlockSpec(
            (pl.Element(cols), pl.Element(block), pl.Element(block)),
            lambda g, b, i: (b[g * group + rr], 0, 0))

    kernel = functools.partial(sparse_kernel, n_w=n_w, group=group, cols=cols, block=block)
    flops = 2 * t * block * block * rows * cols * n_w
    bytes_accessed = x.size * 2 + n_w * (rows * cols * block * block * 2 + t * cols * block * 2)
    return pl.pallas_call(
        kernel,
        grid_spec=pltpu.PrefetchScalarGridSpec(
            num_scalar_prefetch=2,
            grid=(rows // group,),
            in_specs=[pl.BlockSpec((t, group * block), lambda g, b, i: (0, g))]
            + [w_spec(rr) for _ in range(n_w) for rr in range(group)],
            out_specs=[pl.BlockSpec((t, cols * block), lambda g, b, i: (0, 0))] * n_w,
            scratch_shapes=[pltpu.VMEM((t, cols * block), jnp.float32)] * n_w
            + [pltpu.VMEM((group * block, cols * block), jnp.bfloat16)] * n_w,
        ),
        out_shape=[jax.ShapeDtypeStruct((t, cols * block), jnp.bfloat16)] * n_w,
        compiler_params=pltpu.CompilerParams(dimension_semantics=("arbitrary",)),
        cost_estimate=pl.CostEstimate(flops=flops, transcendentals=0, bytes_accessed=bytes_accessed),
    )(base, index, x, *[p for p in packed for _ in range(group)])


def exchange(x, axis, n, bit):
    pairs = [(i, i ^ (1 << bit)) for i in range(n)]
    return lax.ppermute(x, axis, perm=pairs)


def halving_scatter(parts, axis, n, bits):
    me = lax.axis_index(axis)
    for bit in bits:
        half = parts[0].shape[0] // 2
        mine = (me >> bit) & 1
        keep = [lax.dynamic_slice_in_dim(p, mine * half, half, axis=0) for p in parts]
        send = [lax.dynamic_slice_in_dim(p, (1 - mine) * half, half, axis=0) for p in parts]
        got = exchange(tuple(s.astype(jnp.bfloat16) for s in send), axis, n, bit)
        parts = [k.astype(jnp.float32) + g.astype(jnp.float32) for k, g in zip(keep, got)]
    return parts


def doubling_gather(x, axis, n, bits):
    me = lax.axis_index(axis)
    for bit in bits:
        got = exchange(x, axis, n, bit)
        low = ((me >> bit) & 1) == 0
        x = jnp.where(low, jnp.concatenate([x, got], 0), jnp.concatenate([got, x], 0))
    return x


def local(tokens, gate_packed, up_packed, down_packed, gate_keep, down_keep):
    n_row = lax.axis_size("row")
    n_col = lax.axis_size("col")
    row_bits = list(range(n_row.bit_length() - 1))
    col_bits = list(range(n_col.bit_length() - 1))
    segment = doubling_gather(tokens, "col", n_col, col_bits[::-1])
    gate_rows, up_rows = sparse_matmul(segment, [gate_packed, up_packed], gate_keep)
    gate_sum, up_sum = halving_scatter([gate_rows, up_rows], "row", n_row, row_bits)
    hidden_share = (jax.nn.silu(gate_sum) * up_sum).astype(jnp.bfloat16)
    every_hidden = doubling_gather(hidden_share, "row", n_row, row_bits[::-1])
    (partial_out,) = sparse_matmul(every_hidden, [down_packed], down_keep)
    (summed,) = halving_scatter([partial_out], "col", n_col, col_bits)
    return summed.astype(jnp.bfloat16)


def solution(mesh):
    in_specs = (
        P("col", "row"),
        P("row", "col", None),
        P("row", "col", None),
        P("col", "row", None),
        P("row", "col"),
        P("col", "row"),
    )
    out_specs = P("col", "row")
    return jax.shard_map(local, mesh=mesh, in_specs=in_specs, out_specs=out_specs, check_vma=False)
```

```python
import functools

import jax
import jax.numpy as jnp
from jax import lax
from jax.experimental import pallas as pl
from jax.experimental.pallas import tpu as pltpu
from jax.sharding import PartitionSpec as P


def slot_tables(keep, cap):
    rows, cols = keep.shape
    flat = keep.reshape(-1).astype(jnp.int32)
    slot = (jnp.cumsum(flat) - flat).reshape(rows, cols)
    base = jnp.minimum(slot[:, 0], cap - cols)
    index = jnp.where(keep == 1, slot - base[:, None], -1)
    return base.astype(jnp.int32), index.reshape(-1).astype(jnp.int32)


def sparse_kernel(base_ref, index_ref, x_ref, *refs, n_w, group, cols, block):
    w_refs = refs[:n_w * group]
    o_refs = refs[n_w * group:n_w * group + n_w]
    acc_refs = refs[n_w * group + n_w:n_w * group + 2 * n_w]
    panel_refs = refs[n_w * group + 2 * n_w:]
    g = pl.program_id(0)

    @pl.when(g == 0)
    def _():
        for acc in acc_refs:
            acc[...] = jnp.zeros(acc.shape, acc.dtype)

    for rr in range(group):
        for c in range(cols):
            k = index_ref[(g * group + rr) * cols + c]
            for a in range(n_w):
                blk = w_refs[a * group + rr][jnp.maximum(k, 0)]
                panel_refs[a][rr * block:(rr + 1) * block, c * block:(c + 1) * block] = jnp.where(
                    k >= 0, blk, jnp.zeros_like(blk))

    x = x_ref[...]
    for panel, acc in zip(panel_refs, acc_refs):
        acc[...] += jnp.dot(x, panel[...], preferred_element_type=jnp.float32)

    @pl.when(g == pl.num_programs(0) - 1)
    def _():
        for o, acc in zip(o_refs, acc_refs):
            o[...] = acc[...].astype(o.dtype)


def sparse_matmul(x, packed, keep):
    rows, cols = keep.shape
    cap, block, _ = packed[0].shape
    t = x.shape[0]
    n_w = len(packed)
    group = next(s for s in (4, 2, 1) if rows % s == 0)
    base, index = slot_tables(keep, cap)

    def w_spec(rr):
        return pl.BlockSpec(
            (pl.Element(cols), pl.Element(block), pl.Element(block)),
            lambda g, b, i: (b[g * group + rr], 0, 0))

    kernel = functools.partial(sparse_kernel, n_w=n_w, group=group, cols=cols, block=block)
    flops = 2 * t * block * block * rows * cols * n_w
    bytes_accessed = x.size * 2 + n_w * (rows * cols * block * block * 2 + t * cols * block * 2)
    return pl.pallas_call(
        kernel,
        grid_spec=pltpu.PrefetchScalarGridSpec(
            num_scalar_prefetch=2,
            grid=(rows // group,),
            in_specs=[pl.BlockSpec((t, group * block), lambda g, b, i: (0, g))]
            + [w_spec(rr) for _ in range(n_w) for rr in range(group)],
            out_specs=[pl.BlockSpec((t, cols * block), lambda g, b, i: (0, 0))] * n_w,
            scratch_shapes=[pltpu.VMEM((t, cols * block), jnp.float32)] * n_w
            + [pltpu.VMEM((group * block, cols * block), jnp.bfloat16)] * n_w,
        ),
        out_shape=[jax.ShapeDtypeStruct((t, cols * block), jnp.bfloat16)] * n_w,
        compiler_params=pltpu.CompilerParams(dimension_semantics=("arbitrary",)),
        cost_estimate=pl.CostEstimate(flops=flops, transcendentals=0, bytes_accessed=bytes_accessed),
    )(base, index, x, *[p for p in packed for _ in range(group)])


def exchange(x, axis, n, bit):
    pairs = [(i, i ^ (1 << bit)) for i in range(n)]
    return lax.ppermute(x, axis, perm=pairs)


def halving_scatter(streams, axis, n):
    me = lax.axis_index(axis)
    streams = [(list(parts), bits) for parts, bits in streams]
    for step in range(len(streams[0][1])):
        for parts, bits in streams:
            bit = bits[step]
            half = parts[0].shape[0] // 2
            mine = (me >> bit) & 1
            keep = [lax.dynamic_slice_in_dim(p, mine * half, half, axis=0) for p in parts]
            send = [lax.dynamic_slice_in_dim(p, (1 - mine) * half, half, axis=0) for p in parts]
            got = exchange(tuple(s.astype(jnp.bfloat16) for s in send), axis, n, bit)
            parts[:] = [k.astype(jnp.float32) + g.astype(jnp.float32) for k, g in zip(keep, got)]
    return [parts for parts, _ in streams]


def doubling_gather(streams, axis, n):
    me = lax.axis_index(axis)
    xs = [x for x, _ in streams]
    for step in range(len(streams[0][1])):
        for p, (_, bits) in enumerate(streams):
            bit = bits[step]
            got = exchange(xs[p], axis, n, bit)
            low = ((me >> bit) & 1) == 0
            xs[p] = jnp.where(low, jnp.concatenate([xs[p], got], 0), jnp.concatenate([got, xs[p]], 0))
    return xs


def local(tokens, gate_packed, up_packed, down_packed, gate_keep, down_keep):
    n_row = lax.axis_size("row")
    n_col = lax.axis_size("col")
    row_bits = list(range(n_row.bit_length() - 1))
    top = n_col.bit_length() - 1
    col_orders = [list(range(top - 1, -1, -1)), [0] + list(range(top - 1, 0, -1))]
    t_half = tokens.shape[0] // 2
    token_parts = [tokens[:t_half], tokens[t_half:]]
    segment = jnp.concatenate(
        doubling_gather(list(zip(token_parts, col_orders)), "col", n_col), axis=0)
    gate_rows, up_rows = sparse_matmul(segment, [gate_packed, up_packed], gate_keep)
    ((gate_sum, up_sum),) = halving_scatter([([gate_rows, up_rows], row_bits)], "row", n_row)
    hidden_share = (jax.nn.silu(gate_sum) * up_sum).astype(jnp.bfloat16)
    (every_hidden,) = doubling_gather([(hidden_share, row_bits[::-1])], "row", n_row)
    (partial_out,) = sparse_matmul(every_hidden, [down_packed], down_keep)
    half_rows = partial_out.shape[0] // 2
    out_parts = halving_scatter(
        [([partial_out[:half_rows]], col_orders[0][::-1]), ([partial_out[half_rows:]], col_orders[1][::-1])],
        "col", n_col)
    summed = jnp.concatenate([parts[0] for parts in out_parts], axis=0)
    return summed.astype(jnp.bfloat16)


def solution(mesh):
    in_specs = (
        P("col", "row"),
        P("row", "col", None),
        P("row", "col", None),
        P("col", "row", None),
        P("row", "col"),
        P("col", "row"),
    )
    out_specs = P("col", "row")
    return jax.shard_map(local, mesh=mesh, in_specs=in_specs, out_specs=out_specs, check_vma=False)
```

```python
import functools

import jax
import jax.numpy as jnp
from jax import lax
from jax.experimental import pallas as pl
from jax.experimental.pallas import tpu as pltpu
from jax.sharding import PartitionSpec as P


def slot_tables(keep, cap, r0, r1, c0, c1):
    flat = keep.reshape(-1).astype(jnp.int32)
    slot = (jnp.cumsum(flat) - flat).reshape(keep.shape)[r0:r1, c0:c1]
    base = jnp.minimum(slot[:, 0], cap - (c1 - c0))
    index = jnp.where(keep[r0:r1, c0:c1] == 1, slot - base[:, None], -1)
    return base.astype(jnp.int32), index.reshape(-1).astype(jnp.int32)


def sparse_kernel(base_ref, index_ref, x_ref, *refs, n_w, group, cols, block, seeded):
    if seeded:
        init_ref, refs = refs[0], refs[1:]
    w_refs = refs[:n_w * group]
    o_refs = refs[n_w * group:n_w * group + n_w]
    acc_refs = refs[n_w * group + n_w:n_w * group + 2 * n_w]
    panel_refs = refs[n_w * group + 2 * n_w:]
    g = pl.program_id(0)

    @pl.when(g == 0)
    def _():
        for acc in acc_refs:
            acc[...] = init_ref[...] if seeded else jnp.zeros(acc.shape, acc.dtype)

    for rr in range(group):
        for c in range(cols):
            k = index_ref[(g * group + rr) * cols + c]
            for a in range(n_w):
                blk = w_refs[a * group + rr][jnp.maximum(k, 0)]
                panel_refs[a][rr * block:(rr + 1) * block, c * block:(c + 1) * block] = jnp.where(
                    k >= 0, blk, jnp.zeros_like(blk))

    x = x_ref[...]
    for panel, acc in zip(panel_refs, acc_refs):
        acc[...] += jnp.dot(x, panel[...], preferred_element_type=jnp.float32)

    @pl.when(g == pl.num_programs(0) - 1)
    def _():
        for o, acc in zip(o_refs, acc_refs):
            o[...] = acc[...].astype(o.dtype)


def sparse_matmul(x, packed, keep, r0, r1, c0, c1, init=None, out_dtype=jnp.bfloat16):
    rows, cols = r1 - r0, c1 - c0
    cap, block, _ = packed[0].shape
    t = x.shape[0]
    n_w = len(packed)
    group = next(s for s in (4, 2, 1) if rows % s == 0)
    base, index = slot_tables(keep, cap, r0, r1, c0, c1)

    def w_spec(rr):
        return pl.BlockSpec(
            (pl.Element(cols), pl.Element(block), pl.Element(block)),
            lambda g, b, i: (b[g * group + rr], 0, 0))

    seeded = init is not None
    kernel = functools.partial(
        sparse_kernel, n_w=n_w, group=group, cols=cols, block=block, seeded=seeded)
    whole = pl.BlockSpec((t, cols * block), lambda g, b, i: (0, 0))
    flops = 2 * t * block * block * rows * cols * n_w
    bytes_accessed = x.size * 2 + n_w * (rows * cols * block * block * 2 + t * cols * block * 4)
    return pl.pallas_call(
        kernel,
        grid_spec=pltpu.PrefetchScalarGridSpec(
            num_scalar_prefetch=2,
            grid=(rows // group,),
            in_specs=[pl.BlockSpec((t, group * block), lambda g, b, i: (0, g))]
            + ([whole] if seeded else [])
            + [w_spec(rr) for _ in range(n_w) for rr in range(group)],
            out_specs=[whole] * n_w,
            scratch_shapes=[pltpu.VMEM((t, cols * block), jnp.float32)] * n_w
            + [pltpu.VMEM((group * block, cols * block), jnp.bfloat16)] * n_w,
        ),
        out_shape=[jax.ShapeDtypeStruct((t, cols * block), out_dtype)] * n_w,
        compiler_params=pltpu.CompilerParams(dimension_semantics=("arbitrary",)),
        cost_estimate=pl.CostEstimate(flops=flops, transcendentals=0, bytes_accessed=bytes_accessed),
    )(base, index, x, *([init] if seeded else []), *[p for p in packed for _ in range(group)])


def exchange(x, axis, n, bit):
    pairs = [(i, i ^ (1 << bit)) for i in range(n)]
    return lax.ppermute(x, axis, perm=pairs)


def halving_scatter(streams, axis, n):
    me = lax.axis_index(axis)
    streams = [(list(parts), bits) for parts, bits in streams]
    for step in range(len(streams[0][1])):
        for parts, bits in streams:
            bit = bits[step]
            half = parts[0].shape[0] // 2
            mine = (me >> bit) & 1
            keep = [lax.dynamic_slice_in_dim(p, mine * half, half, axis=0) for p in parts]
            send = [lax.dynamic_slice_in_dim(p, (1 - mine) * half, half, axis=0) for p in parts]
            got = exchange(tuple(s.astype(jnp.bfloat16) for s in send), axis, n, bit)
            parts[:] = [k.astype(jnp.float32) + g.astype(jnp.float32) for k, g in zip(keep, got)]
    return [parts for parts, _ in streams]


def doubling_gather(streams, axis, n):
    me = lax.axis_index(axis)
    xs = [x for x, _ in streams]
    for step in range(len(streams[0][1])):
        for p, (_, bits) in enumerate(streams):
            bit = bits[step]
            got = exchange(xs[p], axis, n, bit)
            low = ((me >> bit) & 1) == 0
            xs[p] = jnp.where(low, jnp.concatenate([xs[p], got], 0), jnp.concatenate([got, xs[p]], 0))
    return xs


def local(tokens, gate_packed, up_packed, down_packed, gate_keep, down_keep):
    n_row = lax.axis_size("row")
    n_col = lax.axis_size("col")
    row_bits = list(range(n_row.bit_length() - 1))
    top = n_col.bit_length() - 1
    col_orders = [list(range(top - 1, -1, -1)), [0] + list(range(top - 1, 0, -1))]
    t_half = tokens.shape[0] // 2
    token_parts = [tokens[:t_half], tokens[t_half:]]
    segment = jnp.concatenate(
        doubling_gather(list(zip(token_parts, col_orders)), "col", n_col), axis=0)
    n_in, n_hid = gate_keep.shape
    n_out = down_keep.shape[1]
    split = (n_hid // 2) // 4 * 4 or n_hid // 2
    spans = [(0, split), (split, n_hid)]
    hidden = []
    for h0, h1 in spans:
        gate_rows, up_rows = sparse_matmul(segment, [gate_packed, up_packed], gate_keep, 0, n_in, h0, h1)
        ((gate_sum, up_sum),) = halving_scatter([([gate_rows, up_rows], row_bits)], "row", n_row)
        hidden_share = (jax.nn.silu(gate_sum) * up_sum).astype(jnp.bfloat16)
        hidden += doubling_gather([(hidden_share, row_bits[::-1])], "row", n_row)
    (first_out,) = sparse_matmul(
        hidden[0], [down_packed], down_keep, 0, split, 0, n_out, out_dtype=jnp.float32)
    (partial_out,) = sparse_matmul(
        hidden[1], [down_packed], down_keep, split, n_hid, 0, n_out, init=first_out)
    half_rows = partial_out.shape[0] // 2
    out_parts = halving_scatter(
        [([partial_out[:half_rows]], col_orders[0][::-1]), ([partial_out[half_rows:]], col_orders[1][::-1])],
        "col", n_col)
    summed = jnp.concatenate([parts[0] for parts in out_parts], axis=0)
    return summed.astype(jnp.bfloat16)


def solution(mesh):
    in_specs = (
        P("col", "row"),
        P("row", "col", None),
        P("row", "col", None),
        P("col", "row", None),
        P("row", "col"),
        P("col", "row"),
    )
    out_specs = P("col", "row")
    return jax.shard_map(local, mesh=mesh, in_specs=in_specs, out_specs=out_specs, check_vma=False)
```

```python
import functools

import jax
import jax.numpy as jnp
from jax import lax
from jax.experimental import pallas as pl
from jax.experimental.pallas import tpu as pltpu
from jax.sharding import PartitionSpec as P


def slot_tables(keep, cap):
    rows, cols = keep.shape
    flat = keep.reshape(-1).astype(jnp.int32)
    slot = (jnp.cumsum(flat) - flat).reshape(rows, cols)
    base = jnp.minimum(slot[:, 0], cap - cols)
    index = jnp.where(keep == 1, slot - base[:, None], -1)
    return base.astype(jnp.int32), index.reshape(-1).astype(jnp.int32)


def sparse_kernel(base_ref, index_ref, x_ref, *refs, n_w, group, cols, block):
    w_refs = refs[:n_w * group]
    o_refs = refs[n_w * group:n_w * group + n_w]
    acc_refs = refs[n_w * group + n_w:n_w * group + 2 * n_w]
    panel_refs = refs[n_w * group + 2 * n_w:]
    g = pl.program_id(0)

    @pl.when(g == 0)
    def _():
        for acc in acc_refs:
            acc[...] = jnp.zeros(acc.shape, acc.dtype)

    for rr in range(group):
        for c in range(cols):
            k = index_ref[(g * group + rr) * cols + c]
            for a in range(n_w):
                blk = w_refs[a * group + rr][jnp.maximum(k, 0)]
                panel_refs[a][rr * block:(rr + 1) * block, c * block:(c + 1) * block] = jnp.where(
                    k >= 0, blk, jnp.zeros_like(blk))

    x = x_ref[...]
    for panel, acc in zip(panel_refs, acc_refs):
        acc[...] += jnp.dot(x, panel[...], preferred_element_type=jnp.float32)

    @pl.when(g == pl.num_programs(0) - 1)
    def _():
        for o, acc in zip(o_refs, acc_refs):
            o[...] = acc[...].astype(o.dtype)


def sparse_matmul(x, packed, keep):
    rows, cols = keep.shape
    cap, block, _ = packed[0].shape
    t = x.shape[0]
    n_w = len(packed)
    group = next(s for s in (4, 2, 1) if rows % s == 0)
    base, index = slot_tables(keep, cap)

    def w_spec(rr):
        return pl.BlockSpec(
            (pl.Element(cols), pl.Element(block), pl.Element(block)),
            lambda g, b, i: (b[g * group + rr], 0, 0))

    kernel = functools.partial(sparse_kernel, n_w=n_w, group=group, cols=cols, block=block)
    flops = 2 * t * block * block * rows * cols * n_w
    bytes_accessed = x.size * 2 + n_w * (rows * cols * block * block * 2 + t * cols * block * 2)
    return pl.pallas_call(
        kernel,
        grid_spec=pltpu.PrefetchScalarGridSpec(
            num_scalar_prefetch=2,
            grid=(rows // group,),
            in_specs=[pl.BlockSpec((t, group * block), lambda g, b, i: (0, g))]
            + [w_spec(rr) for _ in range(n_w) for rr in range(group)],
            out_specs=[pl.BlockSpec((t, cols * block), lambda g, b, i: (0, 0))] * n_w,
            scratch_shapes=[pltpu.VMEM((t, cols * block), jnp.float32)] * n_w
            + [pltpu.VMEM((group * block, cols * block), jnp.bfloat16)] * n_w,
        ),
        out_shape=[jax.ShapeDtypeStruct((t, cols * block), jnp.bfloat16)] * n_w,
        compiler_params=pltpu.CompilerParams(dimension_semantics=("arbitrary",)),
        cost_estimate=pl.CostEstimate(flops=flops, transcendentals=0, bytes_accessed=bytes_accessed),
    )(base, index, x, *[p for p in packed for _ in range(group)])


def densify_kernel(base_ref, index_ref, *refs, group, cols, block):
    w_refs = refs[:group]
    o_ref = refs[group]
    g = pl.program_id(0)
    for rr in range(group):
        for c in range(cols):
            k = index_ref[(g * group + rr) * cols + c]
            blk = w_refs[rr][jnp.maximum(k, 0)]
            o_ref[rr * block:(rr + 1) * block, c * block:(c + 1) * block] = jnp.where(
                k >= 0, blk, jnp.zeros_like(blk))


def densify(packed, keep):
    rows, cols = keep.shape
    cap, block, _ = packed.shape
    group = next(s for s in (4, 2, 1) if rows % s == 0)
    base, index = slot_tables(keep, cap)

    def w_spec(rr):
        return pl.BlockSpec(
            (pl.Element(cols), pl.Element(block), pl.Element(block)),
            lambda g, b, i: (b[g * group + rr], 0, 0))

    kernel = functools.partial(densify_kernel, group=group, cols=cols, block=block)
    n_bytes = 2 * rows * cols * block * block * 2
    return pl.pallas_call(
        kernel,
        grid_spec=pltpu.PrefetchScalarGridSpec(
            num_scalar_prefetch=2,
            grid=(rows // group,),
            in_specs=[w_spec(rr) for rr in range(group)],
            out_specs=pl.BlockSpec((group * block, cols * block), lambda g, b, i: (g, 0)),
        ),
        out_shape=jax.ShapeDtypeStruct((rows * block, cols * block), packed.dtype),
        compiler_params=pltpu.CompilerParams(dimension_semantics=("arbitrary",)),
        cost_estimate=pl.CostEstimate(flops=0, transcendentals=0, bytes_accessed=n_bytes),
    )(base, index, *[packed] * group)


def dense_kernel(x_ref, *refs, n_w):
    for w_ref, o_ref in zip(refs[:n_w], refs[n_w:]):
        o_ref[...] = jnp.dot(x_ref[...], w_ref[...], preferred_element_type=jnp.float32).astype(o_ref.dtype)


def dense_matmul(x, ws):
    t, k = x.shape
    n = ws[0].shape[1]
    tn = next(s for s in (512, 256, 128) if n % s == 0)
    n_w = len(ws)
    return pl.pallas_call(
        functools.partial(dense_kernel, n_w=n_w),
        grid=(n // tn,),
        in_specs=[pl.BlockSpec((t, k), lambda j: (0, 0))] + [pl.BlockSpec((k, tn), lambda j: (0, j))] * n_w,
        out_specs=[pl.BlockSpec((t, tn), lambda j: (0, j))] * n_w,
        out_shape=[jax.ShapeDtypeStruct((t, n), jnp.bfloat16)] * n_w,
        compiler_params=pltpu.CompilerParams(dimension_semantics=("arbitrary",)),
        cost_estimate=pl.CostEstimate(
            flops=2 * t * k * n * n_w, transcendentals=0,
            bytes_accessed=x.size * 2 + n_w * (k * n * 2 + t * n * 2)),
    )(x, *ws)


def exchange(x, axis, n, bit):
    pairs = [(i, i ^ (1 << bit)) for i in range(n)]
    return lax.ppermute(x, axis, perm=pairs)


def halving_scatter(streams, axis, n):
    me = lax.axis_index(axis)
    streams = [(list(parts), bits) for parts, bits in streams]
    for step in range(len(streams[0][1])):
        for parts, bits in streams:
            bit = bits[step]
            half = parts[0].shape[0] // 2
            mine = (me >> bit) & 1
            keep = [lax.dynamic_slice_in_dim(p, mine * half, half, axis=0) for p in parts]
            send = [lax.dynamic_slice_in_dim(p, (1 - mine) * half, half, axis=0) for p in parts]
            got = exchange(tuple(s.astype(jnp.bfloat16) for s in send), axis, n, bit)
            parts[:] = [k.astype(jnp.float32) + g.astype(jnp.float32) for k, g in zip(keep, got)]
    return [parts for parts, _ in streams]


def doubling_gather(streams, axis, n):
    me = lax.axis_index(axis)
    xs = [x for x, _ in streams]
    for step in range(len(streams[0][1])):
        for p, (_, bits) in enumerate(streams):
            bit = bits[step]
            got = exchange(xs[p], axis, n, bit)
            low = ((me >> bit) & 1) == 0
            xs[p] = jnp.where(low, jnp.concatenate([xs[p], got], 0), jnp.concatenate([got, xs[p]], 0))
    return xs


def local(tokens, gate_packed, up_packed, down_packed, gate_keep, down_keep):
    n_row = lax.axis_size("row")
    n_col = lax.axis_size("col")
    row_bits = list(range(n_row.bit_length() - 1))
    top = n_col.bit_length() - 1
    col_orders = [list(range(top - 1, -1, -1)), [0] + list(range(top - 1, 0, -1))]
    t_half = tokens.shape[0] // 2
    token_parts = [tokens[:t_half], tokens[t_half:]]
    segment = jnp.concatenate(
        doubling_gather(list(zip(token_parts, col_orders)), "col", n_col), axis=0)
    gate_rows, up_rows = dense_matmul(segment, [densify(gate_packed, gate_keep), densify(up_packed, gate_keep)])
    ((gate_sum, up_sum),) = halving_scatter([([gate_rows, up_rows], row_bits)], "row", n_row)
    hidden_share = (jax.nn.silu(gate_sum) * up_sum).astype(jnp.bfloat16)
    (every_hidden,) = doubling_gather([(hidden_share, row_bits[::-1])], "row", n_row)
    (partial_out,) = dense_matmul(every_hidden, [densify(down_packed, down_keep)])
    half_rows = partial_out.shape[0] // 2
    out_parts = halving_scatter(
        [([partial_out[:half_rows]], col_orders[0][::-1]), ([partial_out[half_rows:]], col_orders[1][::-1])],
        "col", n_col)
    summed = jnp.concatenate([parts[0] for parts in out_parts], axis=0)
    return summed.astype(jnp.bfloat16)


def solution(mesh):
    in_specs = (
        P("col", "row"),
        P("row", "col", None),
        P("row", "col", None),
        P("col", "row", None),
        P("row", "col"),
        P("col", "row"),
    )
    out_specs = P("col", "row")
    return jax.shard_map(local, mesh=mesh, in_specs=in_specs, out_specs=out_specs, check_vma=False)
```

```python
import functools

import jax
import jax.numpy as jnp
from jax import lax
from jax.experimental import pallas as pl
from jax.experimental.pallas import tpu as pltpu
from jax.sharding import PartitionSpec as P


def slot_tables(keep, cap):
    rows, cols = keep.shape
    flat = keep.reshape(-1).astype(jnp.int32)
    slot = (jnp.cumsum(flat) - flat).reshape(rows, cols)
    base = jnp.minimum(slot[:, 0], cap - cols)
    index = jnp.where(keep == 1, slot - base[:, None], -1)
    return base.astype(jnp.int32), index.reshape(-1).astype(jnp.int32)


def sparse_kernel(base_ref, index_ref, x_ref, *refs, n_w, group, cols, block):
    w_refs = refs[:n_w * group]
    o_refs = refs[n_w * group:n_w * group + n_w]
    acc_refs = refs[n_w * group + n_w:n_w * group + 2 * n_w]
    panel_refs = refs[n_w * group + 2 * n_w:]
    g = pl.program_id(0)

    @pl.when(g == 0)
    def _():
        for acc in acc_refs:
            acc[...] = jnp.zeros(acc.shape, acc.dtype)

    for rr in range(group):
        for c in range(cols):
            k = index_ref[(g * group + rr) * cols + c]
            for a in range(n_w):
                blk = w_refs[a * group + rr][jnp.maximum(k, 0)]
                panel_refs[a][rr * block:(rr + 1) * block, c * block:(c + 1) * block] = jnp.where(
                    k >= 0, blk, jnp.zeros_like(blk))

    x = x_ref[...]
    for panel, acc in zip(panel_refs, acc_refs):
        acc[...] += jnp.dot(x, panel[...], preferred_element_type=jnp.float32)

    @pl.when(g == pl.num_programs(0) - 1)
    def _():
        for o, acc in zip(o_refs, acc_refs):
            o[...] = acc[...].astype(o.dtype)


def sparse_matmul(x, packed, keep):
    rows, cols = keep.shape
    cap, block, _ = packed[0].shape
    t = x.shape[0]
    n_w = len(packed)
    group = next(s for s in (4, 2, 1) if rows % s == 0)
    base, index = slot_tables(keep, cap)

    def w_spec(rr):
        return pl.BlockSpec(
            (pl.Element(cols), pl.Element(block), pl.Element(block)),
            lambda g, b, i: (b[g * group + rr], 0, 0))

    kernel = functools.partial(sparse_kernel, n_w=n_w, group=group, cols=cols, block=block)
    flops = 2 * t * block * block * rows * cols * n_w
    bytes_accessed = x.size * 2 + n_w * (rows * cols * block * block * 2 + t * cols * block * 2)
    return pl.pallas_call(
        kernel,
        grid_spec=pltpu.PrefetchScalarGridSpec(
            num_scalar_prefetch=2,
            grid=(rows // group,),
            in_specs=[pl.BlockSpec((t, group * block), lambda g, b, i: (0, g))]
            + [w_spec(rr) for _ in range(n_w) for rr in range(group)],
            out_specs=[pl.BlockSpec((t, cols * block), lambda g, b, i: (0, 0))] * n_w,
            scratch_shapes=[pltpu.VMEM((t, cols * block), jnp.float32)] * n_w
            + [pltpu.VMEM((group * block, cols * block), jnp.bfloat16)] * n_w,
        ),
        out_shape=[jax.ShapeDtypeStruct((t, cols * block), jnp.bfloat16)] * n_w,
        compiler_params=pltpu.CompilerParams(dimension_semantics=("arbitrary",)),
        cost_estimate=pl.CostEstimate(flops=flops, transcendentals=0, bytes_accessed=bytes_accessed),
    )(base, index, x, *[p for p in packed for _ in range(group)])


def exchange(x, axis, n, bit):
    pairs = [(i, i ^ (1 << bit)) for i in range(n)]
    return lax.ppermute(x, axis, perm=pairs)


def halving_scatter(streams, axis, n):
    me = lax.axis_index(axis)
    streams = [(list(parts), bits) for parts, bits in streams]
    for step in range(len(streams[0][1])):
        for parts, bits in streams:
            bit = bits[step]
            half = parts[0].shape[0] // 2
            mine = (me >> bit) & 1
            keep = [lax.dynamic_slice_in_dim(p, mine * half, half, axis=0) for p in parts]
            send = [lax.dynamic_slice_in_dim(p, (1 - mine) * half, half, axis=0) for p in parts]
            got = exchange(tuple(s.astype(jnp.bfloat16) for s in send), axis, n, bit)
            parts[:] = [k.astype(jnp.float32) + g.astype(jnp.float32) for k, g in zip(keep, got)]
    return [parts for parts, _ in streams]


def doubling_gather(streams, axis, n):
    me = lax.axis_index(axis)
    xs = [x for x, _ in streams]
    for step in range(len(streams[0][1])):
        for p, (_, bits) in enumerate(streams):
            bit = bits[step]
            got = exchange(xs[p], axis, n, bit)
            low = ((me >> bit) & 1) == 0
            xs[p] = jnp.where(low, jnp.concatenate([xs[p], got], 0), jnp.concatenate([got, xs[p]], 0))
    return xs


def local(tokens, gate_packed, up_packed, down_packed, gate_keep, down_keep):
    n_row = lax.axis_size("row")
    n_col = lax.axis_size("col")
    row_bits = list(range(n_row.bit_length() - 1))
    top = n_col.bit_length() - 1
    col_orders = [list(range(top - 1, -1, -1)), [0] + list(range(top - 1, 0, -1))]
    quarter = tokens.shape[0] // 4
    orders = col_orders * 2
    token_parts = [tokens[q * quarter:(q + 1) * quarter] for q in range(4)]
    segment = jnp.concatenate(doubling_gather(list(zip(token_parts, orders)), "col", n_col), axis=0)
    gate_rows, up_rows = sparse_matmul(segment, [gate_packed, up_packed], gate_keep)
    half = segment.shape[0] // 2
    results = []
    held = None
    for h in range(2):
        gate_h, up_h = gate_rows[h * half:(h + 1) * half], up_rows[h * half:(h + 1) * half]
        if held is not None:
            held, gate_h, up_h = lax.optimization_barrier((held, gate_h, up_h))
        ((gate_sum, up_sum),) = halving_scatter([([gate_h, up_h], row_bits)], "row", n_row)
        hidden_share = (jax.nn.silu(gate_sum) * up_sum).astype(jnp.bfloat16)
        (hidden,) = doubling_gather([(hidden_share, row_bits[::-1])], "row", n_row)
        held = hidden
        (partial_out,) = sparse_matmul(hidden, [down_packed], down_keep)
        out_parts = halving_scatter(
            [([partial_out[:half // 2]], orders[2 * h][::-1]),
             ([partial_out[half // 2:]], orders[2 * h + 1][::-1])],
            "col", n_col)
        results += [parts[0] for parts in out_parts]
    return jnp.concatenate(results, axis=0).astype(jnp.bfloat16)


def solution(mesh):
    in_specs = (
        P("col", "row"),
        P("row", "col", None),
        P("row", "col", None),
        P("col", "row", None),
        P("row", "col"),
        P("col", "row"),
    )
    out_specs = P("col", "row")
    return jax.shard_map(local, mesh=mesh, in_specs=in_specs, out_specs=out_specs, check_vma=False)
```

```python
import functools

import jax
import jax.numpy as jnp
from jax import lax
from jax.experimental import pallas as pl
from jax.experimental.pallas import tpu as pltpu
from jax.sharding import PartitionSpec as P


def slot_tables(keep, cap):
    rows, cols = keep.shape
    flat = keep.reshape(-1).astype(jnp.int32)
    slot = (jnp.cumsum(flat) - flat).reshape(rows, cols)
    base = jnp.minimum(slot[:, 0], cap - cols)
    index = jnp.where(keep == 1, slot - base[:, None], -1)
    return base.astype(jnp.int32), index.reshape(-1).astype(jnp.int32)


def sparse_kernel(base_ref, index_ref, x_ref, *refs, n_w, group, cols, block):
    w_refs = refs[:n_w * group]
    o_refs = refs[n_w * group:n_w * group + n_w]
    acc_refs = refs[n_w * group + n_w:n_w * group + 2 * n_w]
    panel_refs = refs[n_w * group + 2 * n_w:]
    g = pl.program_id(0)

    @pl.when(g == 0)
    def _():
        for acc in acc_refs:
            acc[...] = jnp.zeros(acc.shape, acc.dtype)

    for rr in range(group):
        for c in range(cols):
            k = index_ref[(g * group + rr) * cols + c]
            for a in range(n_w):
                blk = w_refs[a * group + rr][jnp.maximum(k, 0)]
                panel_refs[a][rr * block:(rr + 1) * block, c * block:(c + 1) * block] = jnp.where(
                    k >= 0, blk, jnp.zeros_like(blk))

    x = x_ref[...]
    for panel, acc in zip(panel_refs, acc_refs):
        acc[...] += jnp.dot(x, panel[...], preferred_element_type=jnp.float32)

    @pl.when(g == pl.num_programs(0) - 1)
    def _():
        for o, acc in zip(o_refs, acc_refs):
            o[...] = acc[...].astype(o.dtype)


def sparse_matmul(x, packed, keep):
    rows, cols = keep.shape
    cap, block, _ = packed[0].shape
    t = x.shape[0]
    n_w = len(packed)
    group = next(s for s in (4, 2, 1) if rows % s == 0)
    base, index = slot_tables(keep, cap)

    def w_spec(rr):
        return pl.BlockSpec(
            (pl.Element(cols), pl.Element(block), pl.Element(block)),
            lambda g, b, i: (b[g * group + rr], 0, 0))

    kernel = functools.partial(sparse_kernel, n_w=n_w, group=group, cols=cols, block=block)
    flops = 2 * t * block * block * rows * cols * n_w
    bytes_accessed = x.size * 2 + n_w * (rows * cols * block * block * 2 + t * cols * block * 2)
    return pl.pallas_call(
        kernel,
        grid_spec=pltpu.PrefetchScalarGridSpec(
            num_scalar_prefetch=2,
            grid=(rows // group,),
            in_specs=[pl.BlockSpec((t, group * block), lambda g, b, i: (0, g))]
            + [w_spec(rr) for _ in range(n_w) for rr in range(group)],
            out_specs=[pl.BlockSpec((t, cols * block), lambda g, b, i: (0, 0))] * n_w,
            scratch_shapes=[pltpu.VMEM((t, cols * block), jnp.float32)] * n_w
            + [pltpu.VMEM((group * block, cols * block), jnp.bfloat16)] * n_w,
        ),
        out_shape=[jax.ShapeDtypeStruct((t, cols * block), jnp.bfloat16)] * n_w,
        compiler_params=pltpu.CompilerParams(dimension_semantics=("arbitrary",)),
        cost_estimate=pl.CostEstimate(flops=flops, transcendentals=0, bytes_accessed=bytes_accessed),
    )(base, index, x, *[p for p in packed for _ in range(group)])


def exchange(x, axis, n, bit):
    pairs = [(i, i ^ (1 << bit)) for i in range(n)]
    return lax.ppermute(x, axis, perm=pairs)


def halving_scatter(streams, axis, n):
    me = lax.axis_index(axis)
    streams = [(list(parts), bits) for parts, bits in streams]
    for step in range(len(streams[0][1])):
        for parts, bits in streams:
            bit = bits[step]
            half = parts[0].shape[0] // 2
            mine = (me >> bit) & 1
            keep = [lax.dynamic_slice_in_dim(p, mine * half, half, axis=0) for p in parts]
            send = [lax.dynamic_slice_in_dim(p, (1 - mine) * half, half, axis=0) for p in parts]
            got = exchange(tuple(s.astype(jnp.bfloat16) for s in send), axis, n, bit)
            parts[:] = [k.astype(jnp.float32) + g.astype(jnp.float32) for k, g in zip(keep, got)]
    return [parts for parts, _ in streams]


def doubling_gather(streams, axis, n):
    me = lax.axis_index(axis)
    xs = [x for x, _ in streams]
    for step in range(len(streams[0][1])):
        for p, (_, bits) in enumerate(streams):
            bit = bits[step]
            got = exchange(xs[p], axis, n, bit)
            low = ((me >> bit) & 1) == 0
            xs[p] = jnp.where(low, jnp.concatenate([xs[p], got], 0), jnp.concatenate([got, xs[p]], 0))
    return xs


def local(tokens, gate_packed, up_packed, down_packed, gate_keep, down_keep):
    n_row = lax.axis_size("row")
    n_col = lax.axis_size("col")
    row_bits = list(range(n_row.bit_length() - 1))
    top = n_col.bit_length() - 1
    col_orders = [list(range(top - 1, -1, -1)), [0] + list(range(top - 1, 0, -1))]
    t_half = tokens.shape[0] // 2
    token_parts = [tokens[:t_half], tokens[t_half:]]
    segment = jnp.concatenate(
        doubling_gather(list(zip(token_parts, col_orders)), "col", n_col), axis=0)
    gate_rows, up_rows = sparse_matmul(segment, [gate_packed, up_packed], gate_keep)
    half = gate_rows.shape[0] // 2
    sums = halving_scatter(
        [([gate_rows[:half], up_rows[:half]], row_bits), ([gate_rows[half:], up_rows[half:]], row_bits)],
        "row", n_row)
    hidden_shares = [(jax.nn.silu(g) * u).astype(jnp.bfloat16) for g, u in sums]
    every_hidden = jnp.concatenate(
        doubling_gather([(h, row_bits[::-1]) for h in hidden_shares], "row", n_row), axis=0)
    (partial_out,) = sparse_matmul(every_hidden, [down_packed], down_keep)
    half_rows = partial_out.shape[0] // 2
    out_parts = halving_scatter(
        [([partial_out[:half_rows]], col_orders[0][::-1]), ([partial_out[half_rows:]], col_orders[1][::-1])],
        "col", n_col)
    summed = jnp.concatenate([parts[0] for parts in out_parts], axis=0)
    return summed.astype(jnp.bfloat16)


def solution(mesh):
    in_specs = (
        P("col", "row"),
        P("row", "col", None),
        P("row", "col", None),
        P("col", "row", None),
        P("row", "col"),
        P("col", "row"),
    )
    out_specs = P("col", "row")
    return jax.shard_map(local, mesh=mesh, in_specs=in_specs, out_specs=out_specs, check_vma=False)
```

```python
import functools

import jax
import jax.numpy as jnp
from jax import lax
from jax.experimental import pallas as pl
from jax.experimental.pallas import tpu as pltpu
from jax.sharding import PartitionSpec as P


def slot_tables(keep, cap):
    rows, cols = keep.shape
    flat = keep.reshape(-1).astype(jnp.int32)
    slot = (jnp.cumsum(flat) - flat).reshape(rows, cols)
    base = jnp.minimum(slot[:, 0], cap - cols)
    index = jnp.where(keep == 1, slot - base[:, None], -1)
    return base.astype(jnp.int32), index.reshape(-1).astype(jnp.int32)


def sparse_kernel(base_ref, index_ref, x_ref, *refs, n_w, group, cols, block):
    w_refs = refs[:n_w * group]
    o_refs = refs[n_w * group:n_w * group + n_w]
    acc_refs = refs[n_w * group + n_w:n_w * group + 2 * n_w]
    panel_refs = refs[n_w * group + 2 * n_w:]
    g = pl.program_id(0)

    @pl.when(g == 0)
    def _():
        for acc in acc_refs:
            acc[...] = jnp.zeros(acc.shape, acc.dtype)

    for rr in range(group):
        for c in range(cols):
            k = index_ref[(g * group + rr) * cols + c]
            for a in range(n_w):
                blk = w_refs[a * group + rr][jnp.maximum(k, 0)]
                panel_refs[a][rr * block:(rr + 1) * block, c * block:(c + 1) * block] = jnp.where(
                    k >= 0, blk, jnp.zeros_like(blk))

    x = x_ref[...]
    for panel, acc in zip(panel_refs, acc_refs):
        acc[...] += jnp.dot(x, panel[...], preferred_element_type=jnp.float32)

    @pl.when(g == pl.num_programs(0) - 1)
    def _():
        for o, acc in zip(o_refs, acc_refs):
            o[...] = acc[...].astype(o.dtype)


def sparse_matmul(x, packed, keep):
    rows, cols = keep.shape
    cap, block, _ = packed[0].shape
    t = x.shape[0]
    n_w = len(packed)
    group = next(s for s in (4, 2, 1) if rows % s == 0)
    base, index = slot_tables(keep, cap)

    def w_spec(rr):
        return pl.BlockSpec(
            (pl.Element(cols), pl.Element(block), pl.Element(block)),
            lambda g, b, i: (b[g * group + rr], 0, 0))

    kernel = functools.partial(sparse_kernel, n_w=n_w, group=group, cols=cols, block=block)
    flops = 2 * t * block * block * rows * cols * n_w
    bytes_accessed = x.size * 2 + n_w * (rows * cols * block * block * 2 + t * cols * block * 2)
    return pl.pallas_call(
        kernel,
        grid_spec=pltpu.PrefetchScalarGridSpec(
            num_scalar_prefetch=2,
            grid=(rows // group,),
            in_specs=[pl.BlockSpec((t, group * block), lambda g, b, i: (0, g))]
            + [w_spec(rr) for _ in range(n_w) for rr in range(group)],
            out_specs=[pl.BlockSpec((t, cols * block), lambda g, b, i: (0, 0))] * n_w,
            scratch_shapes=[pltpu.VMEM((t, cols * block), jnp.float32)] * n_w
            + [pltpu.VMEM((group * block, cols * block), jnp.bfloat16)] * n_w,
        ),
        out_shape=[jax.ShapeDtypeStruct((t, cols * block), jnp.bfloat16)] * n_w,
        compiler_params=pltpu.CompilerParams(dimension_semantics=("arbitrary",)),
        cost_estimate=pl.CostEstimate(flops=flops, transcendentals=0, bytes_accessed=bytes_accessed),
    )(base, index, x, *[p for p in packed for _ in range(group)])


def exchange(x, axis, n, bit):
    pairs = [(i, i ^ (1 << bit)) for i in range(n)]
    return lax.ppermute(x, axis, perm=pairs)


def halving_scatter(streams, axis, n):
    me = lax.axis_index(axis)
    streams = [(list(parts), bits) for parts, bits in streams]
    for step in range(len(streams[0][1])):
        for parts, bits in streams:
            bit = bits[step]
            half = parts[0].shape[0] // 2
            mine = (me >> bit) & 1
            keep = [lax.dynamic_slice_in_dim(p, mine * half, half, axis=0) for p in parts]
            send = [lax.dynamic_slice_in_dim(p, (1 - mine) * half, half, axis=0) for p in parts]
            got = exchange(tuple(s.astype(jnp.bfloat16) for s in send), axis, n, bit)
            parts[:] = [k.astype(jnp.float32) + g.astype(jnp.float32) for k, g in zip(keep, got)]
    return [parts for parts, _ in streams]


def doubling_gather(streams, axis, n):
    me = lax.axis_index(axis)
    xs = [x for x, _ in streams]
    for step in range(len(streams[0][1])):
        for p, (_, bits) in enumerate(streams):
            bit = bits[step]
            got = exchange(xs[p], axis, n, bit)
            low = ((me >> bit) & 1) == 0
            xs[p] = jnp.where(low, jnp.concatenate([xs[p], got], 0), jnp.concatenate([got, xs[p]], 0))
    return xs


def local(tokens, gate_packed, up_packed, down_packed, gate_keep, down_keep):
    n_row = lax.axis_size("row")
    n_col = lax.axis_size("col")
    row_bits = list(range(n_row.bit_length() - 1))
    top = n_col.bit_length() - 1
    col_orders = [list(range(top - 1, -1, -1)), [0] + list(range(top - 1, 0, -1))]
    quarter = tokens.shape[0] // 4
    orders = col_orders * 2
    token_parts = [tokens[q * quarter:(q + 1) * quarter] for q in range(4)]
    segment = jnp.concatenate(doubling_gather(list(zip(token_parts, orders)), "col", n_col), axis=0)
    gate_rows, up_rows = sparse_matmul(segment, [gate_packed, up_packed], gate_keep)
    half = gate_rows.shape[0] // 2
    sums = halving_scatter(
        [([gate_rows[:half], up_rows[:half]], row_bits), ([gate_rows[half:], up_rows[half:]], row_bits)],
        "row", n_row)
    hidden_shares = [(jax.nn.silu(g) * u).astype(jnp.bfloat16) for g, u in sums]
    every_hidden = jnp.concatenate(
        doubling_gather([(h, row_bits[::-1]) for h in hidden_shares], "row", n_row), axis=0)
    (partial_out,) = sparse_matmul(every_hidden, [down_packed], down_keep)
    rows_q = partial_out.shape[0] // 4
    out_parts = halving_scatter(
        [([partial_out[q * rows_q:(q + 1) * rows_q]], orders[q][::-1]) for q in range(4)], "col", n_col)
    summed = jnp.concatenate([parts[0] for parts in out_parts], axis=0)
    return summed.astype(jnp.bfloat16)


def solution(mesh):
    in_specs = (
        P("col", "row"),
        P("row", "col", None),
        P("row", "col", None),
        P("col", "row", None),
        P("row", "col"),
        P("col", "row"),
    )
    out_specs = P("col", "row")
    return jax.shard_map(local, mesh=mesh, in_specs=in_specs, out_specs=out_specs, check_vma=False)
```

```python
import functools

import jax
import jax.numpy as jnp
from jax import lax
from jax.experimental import pallas as pl
from jax.experimental.pallas import tpu as pltpu
from jax.sharding import PartitionSpec as P


def slot_tables(keep, cap):
    rows, cols = keep.shape
    flat = keep.reshape(-1).astype(jnp.int32)
    slot = (jnp.cumsum(flat) - flat).reshape(rows, cols)
    base = jnp.minimum(slot[:, 0], cap - cols)
    index = jnp.where(keep == 1, slot - base[:, None], -1)
    return base.astype(jnp.int32), index.reshape(-1).astype(jnp.int32)


def sparse_kernel(base_ref, index_ref, x_ref, *refs, n_w, group, cols, block):
    w_refs = refs[:n_w * group]
    o_refs = refs[n_w * group:n_w * group + n_w]
    acc_refs = refs[n_w * group + n_w:n_w * group + 2 * n_w]
    panel_refs = refs[n_w * group + 2 * n_w:]
    g = pl.program_id(0)

    @pl.when(g == 0)
    def _():
        for acc in acc_refs:
            acc[...] = jnp.zeros(acc.shape, acc.dtype)

    for rr in range(group):
        for c in range(cols):
            k = index_ref[(g * group + rr) * cols + c]
            for a in range(n_w):
                blk = w_refs[a * group + rr][jnp.maximum(k, 0)]
                panel_refs[a][rr * block:(rr + 1) * block, c * block:(c + 1) * block] = jnp.where(
                    k >= 0, blk, jnp.zeros_like(blk))

    x = x_ref[...]
    for panel, acc in zip(panel_refs, acc_refs):
        acc[...] += jnp.dot(x, panel[...], preferred_element_type=jnp.float32)

    @pl.when(g == pl.num_programs(0) - 1)
    def _():
        for o, acc in zip(o_refs, acc_refs):
            o[...] = acc[...].astype(o.dtype)


def sparse_matmul(x, packed, keep):
    rows, cols = keep.shape
    cap, block, _ = packed[0].shape
    t = x.shape[0]
    n_w = len(packed)
    group = next(s for s in (4, 2, 1) if rows % s == 0)
    base, index = slot_tables(keep, cap)

    def w_spec(rr):
        return pl.BlockSpec(
            (pl.Element(cols), pl.Element(block), pl.Element(block)),
            lambda g, b, i: (b[g * group + rr], 0, 0))

    kernel = functools.partial(sparse_kernel, n_w=n_w, group=group, cols=cols, block=block)
    flops = 2 * t * block * block * rows * cols * n_w
    bytes_accessed = x.size * 2 + n_w * (rows * cols * block * block * 2 + t * cols * block * 2)
    return pl.pallas_call(
        kernel,
        grid_spec=pltpu.PrefetchScalarGridSpec(
            num_scalar_prefetch=2,
            grid=(rows // group,),
            in_specs=[pl.BlockSpec((t, group * block), lambda g, b, i: (0, g))]
            + [w_spec(rr) for _ in range(n_w) for rr in range(group)],
            out_specs=[pl.BlockSpec((t, cols * block), lambda g, b, i: (0, 0))] * n_w,
            scratch_shapes=[pltpu.VMEM((t, cols * block), jnp.float32)] * n_w
            + [pltpu.VMEM((group * block, cols * block), jnp.bfloat16)] * n_w,
        ),
        out_shape=[jax.ShapeDtypeStruct((t, cols * block), jnp.bfloat16)] * n_w,
        compiler_params=pltpu.CompilerParams(dimension_semantics=("arbitrary",)),
        cost_estimate=pl.CostEstimate(flops=flops, transcendentals=0, bytes_accessed=bytes_accessed),
    )(base, index, x, *[p for p in packed for _ in range(group)])


def exchange(x, axis, n, bit):
    pairs = [(i, i ^ (1 << bit)) for i in range(n)]
    return lax.ppermute(x, axis, perm=pairs)


def halving_scatter(streams, axis, n):
    me = lax.axis_index(axis)
    streams = [(list(parts), bits) for parts, bits in streams]
    for step in range(len(streams[0][1])):
        for parts, bits in streams:
            bit = bits[step]
            half = parts[0].shape[0] // 2
            mine = (me >> bit) & 1
            keep = [lax.dynamic_slice_in_dim(p, mine * half, half, axis=0) for p in parts]
            send = [lax.dynamic_slice_in_dim(p, (1 - mine) * half, half, axis=0) for p in parts]
            got = exchange(tuple(s.astype(jnp.bfloat16) for s in send), axis, n, bit)
            parts[:] = [k.astype(jnp.float32) + g.astype(jnp.float32) for k, g in zip(keep, got)]
    return [parts for parts, _ in streams]


def doubling_gather(streams, axis, n):
    me = lax.axis_index(axis)
    xs = [x for x, _ in streams]
    for step in range(len(streams[0][1])):
        for p, (_, bits) in enumerate(streams):
            bit = bits[step]
            got = exchange(xs[p], axis, n, bit)
            low = ((me >> bit) & 1) == 0
            xs[p] = jnp.where(low, jnp.concatenate([xs[p], got], 0), jnp.concatenate([got, xs[p]], 0))
    return xs


def local(tokens, gate_packed, up_packed, down_packed, gate_keep, down_keep):
    n_row = lax.axis_size("row")
    n_col = lax.axis_size("col")
    row_bits = list(range(n_row.bit_length() - 1))
    top = n_col.bit_length() - 1
    col_orders = [list(range(top - 1, -1, -1)), [0] + list(range(top - 1, 0, -1))]
    quarter = tokens.shape[0] // 4
    orders = col_orders * 2
    token_parts = [tokens[q * quarter:(q + 1) * quarter] for q in range(4)]
    segment = jnp.concatenate(doubling_gather(list(zip(token_parts, orders)), "col", n_col), axis=0)
    gate_rows, up_rows = sparse_matmul(segment, [gate_packed, up_packed], gate_keep)
    rq = gate_rows.shape[0] // 4
    sums = halving_scatter(
        [([gate_rows[q * rq:(q + 1) * rq], up_rows[q * rq:(q + 1) * rq]], row_bits) for q in range(4)],
        "row", n_row)
    hidden_shares = [(jax.nn.silu(g) * u).astype(jnp.bfloat16) for g, u in sums]
    every_hidden = jnp.concatenate(
        doubling_gather([(h, row_bits[::-1]) for h in hidden_shares], "row", n_row), axis=0)
    (partial_out,) = sparse_matmul(every_hidden, [down_packed], down_keep)
    rows_q = partial_out.shape[0] // 4
    out_parts = halving_scatter(
        [([partial_out[q * rows_q:(q + 1) * rows_q]], orders[q][::-1]) for q in range(4)], "col", n_col)
    summed = jnp.concatenate([parts[0] for parts in out_parts], axis=0)
    return summed.astype(jnp.bfloat16)


def solution(mesh):
    in_specs = (
        P("col", "row"),
        P("row", "col", None),
        P("row", "col", None),
        P("col", "row", None),
        P("row", "col"),
        P("col", "row"),
    )
    out_specs = P("col", "row")
    return jax.shard_map(local, mesh=mesh, in_specs=in_specs, out_specs=out_specs, check_vma=False)
```

```python
import functools

import jax
import jax.numpy as jnp
from jax import lax
from jax.experimental import pallas as pl
from jax.experimental.pallas import tpu as pltpu
from jax.sharding import PartitionSpec as P


def slot_tables(keep, cap, r0, r1, c0, c1):
    flat = keep.reshape(-1).astype(jnp.int32)
    slot = (jnp.cumsum(flat) - flat).reshape(keep.shape)[r0:r1, c0:c1]
    base = jnp.minimum(slot[:, 0], cap - (c1 - c0))
    index = jnp.where(keep[r0:r1, c0:c1] == 1, slot - base[:, None], -1)
    return base.astype(jnp.int32), index.reshape(-1).astype(jnp.int32)


def sparse_kernel(base_ref, index_ref, x_ref, *refs, n_w, group, cols, block, seeded):
    if seeded:
        init_ref, refs = refs[0], refs[1:]
    w_refs = refs[:n_w * group]
    o_refs = refs[n_w * group:n_w * group + n_w]
    acc_refs = refs[n_w * group + n_w:n_w * group + 2 * n_w]
    panel_refs = refs[n_w * group + 2 * n_w:]
    g = pl.program_id(0)

    @pl.when(g == 0)
    def _():
        for acc in acc_refs:
            acc[...] = init_ref[...] if seeded else jnp.zeros(acc.shape, acc.dtype)

    for rr in range(group):
        for c in range(cols):
            k = index_ref[(g * group + rr) * cols + c]
            for a in range(n_w):
                blk = w_refs[a * group + rr][jnp.maximum(k, 0)]
                panel_refs[a][rr * block:(rr + 1) * block, c * block:(c + 1) * block] = jnp.where(
                    k >= 0, blk, jnp.zeros_like(blk))

    x = x_ref[...]
    for panel, acc in zip(panel_refs, acc_refs):
        acc[...] += jnp.dot(x, panel[...], preferred_element_type=jnp.float32)

    @pl.when(g == pl.num_programs(0) - 1)
    def _():
        for o, acc in zip(o_refs, acc_refs):
            o[...] = acc[...].astype(o.dtype)


def sparse_matmul(x, packed, keep, r0, r1, c0, c1, init=None, out_dtype=jnp.bfloat16):
    rows, cols = r1 - r0, c1 - c0
    cap, block, _ = packed[0].shape
    t = x.shape[0]
    n_w = len(packed)
    group = next(s for s in (4, 2, 1) if rows % s == 0)
    base, index = slot_tables(keep, cap, r0, r1, c0, c1)

    def w_spec(rr):
        return pl.BlockSpec(
            (pl.Element(cols), pl.Element(block), pl.Element(block)),
            lambda g, b, i: (b[g * group + rr], 0, 0))

    seeded = init is not None
    kernel = functools.partial(
        sparse_kernel, n_w=n_w, group=group, cols=cols, block=block, seeded=seeded)
    whole = pl.BlockSpec((t, cols * block), lambda g, b, i: (0, 0))
    flops = 2 * t * block * block * rows * cols * n_w
    bytes_accessed = x.size * 2 + n_w * (rows * cols * block * block * 2 + t * cols * block * 4)
    return pl.pallas_call(
        kernel,
        grid_spec=pltpu.PrefetchScalarGridSpec(
            num_scalar_prefetch=2,
            grid=(rows // group,),
            in_specs=[pl.BlockSpec((t, group * block), lambda g, b, i: (0, g))]
            + ([whole] if seeded else [])
            + [w_spec(rr) for _ in range(n_w) for rr in range(group)],
            out_specs=[whole] * n_w,
            scratch_shapes=[pltpu.VMEM((t, cols * block), jnp.float32)] * n_w
            + [pltpu.VMEM((group * block, cols * block), jnp.bfloat16)] * n_w,
        ),
        out_shape=[jax.ShapeDtypeStruct((t, cols * block), out_dtype)] * n_w,
        compiler_params=pltpu.CompilerParams(dimension_semantics=("arbitrary",)),
        cost_estimate=pl.CostEstimate(flops=flops, transcendentals=0, bytes_accessed=bytes_accessed),
    )(base, index, x, *([init] if seeded else []), *[p for p in packed for _ in range(group)])


def exchange(x, axis, n, bit):
    pairs = [(i, i ^ (1 << bit)) for i in range(n)]
    return lax.ppermute(x, axis, perm=pairs)


def halving_scatter(streams, axis, n):
    me = lax.axis_index(axis)
    streams = [(list(parts), bits) for parts, bits in streams]
    for step in range(len(streams[0][1])):
        for parts, bits in streams:
            bit = bits[step]
            half = parts[0].shape[0] // 2
            mine = (me >> bit) & 1
            keep = [lax.dynamic_slice_in_dim(p, mine * half, half, axis=0) for p in parts]
            send = [lax.dynamic_slice_in_dim(p, (1 - mine) * half, half, axis=0) for p in parts]
            got = exchange(tuple(s.astype(jnp.bfloat16) for s in send), axis, n, bit)
            parts[:] = [k.astype(jnp.float32) + g.astype(jnp.float32) for k, g in zip(keep, got)]
    return [parts for parts, _ in streams]


def doubling_gather(streams, axis, n):
    me = lax.axis_index(axis)
    xs = [x for x, _ in streams]
    for step in range(len(streams[0][1])):
        for p, (_, bits) in enumerate(streams):
            bit = bits[step]
            got = exchange(xs[p], axis, n, bit)
            low = ((me >> bit) & 1) == 0
            xs[p] = jnp.where(low, jnp.concatenate([xs[p], got], 0), jnp.concatenate([got, xs[p]], 0))
    return xs


def local(tokens, gate_packed, up_packed, down_packed, gate_keep, down_keep):
    n_row = lax.axis_size("row")
    n_col = lax.axis_size("col")
    row_bits = list(range(n_row.bit_length() - 1))
    top = n_col.bit_length() - 1
    col_orders = [list(range(top - 1, -1, -1)), [0] + list(range(top - 1, 0, -1))]
    quarter = tokens.shape[0] // 4
    orders = col_orders * 2
    token_parts = [tokens[q * quarter:(q + 1) * quarter] for q in range(4)]
    segment = jnp.concatenate(doubling_gather(list(zip(token_parts, orders)), "col", n_col), axis=0)
    n_in, n_hid = gate_keep.shape
    gate_rows, up_rows = sparse_matmul(segment, [gate_packed, up_packed], gate_keep, 0, n_in, 0, n_hid)
    half = gate_rows.shape[0] // 2
    sums = halving_scatter(
        [([gate_rows[:half], up_rows[:half]], row_bits), ([gate_rows[half:], up_rows[half:]], row_bits)],
        "row", n_row)
    hidden_shares = [(jax.nn.silu(g) * u).astype(jnp.bfloat16) for g, u in sums]
    every_hidden = jnp.concatenate(
        doubling_gather([(h, row_bits[::-1]) for h in hidden_shares], "row", n_row), axis=0)
    n_out = down_keep.shape[1]
    out_half = n_out // 2
    pieces = []
    for o0, o1 in ((0, out_half), (out_half, n_out)):
        (partial_out,) = sparse_matmul(every_hidden, [down_packed], down_keep, 0, n_hid, o0, o1)
        rows_q = partial_out.shape[0] // 4
        out_parts = halving_scatter(
            [([partial_out[q * rows_q:(q + 1) * rows_q]], orders[q][::-1]) for q in range(4)], "col", n_col)
        pieces.append(jnp.concatenate([parts[0] for parts in out_parts], axis=0))
    return jnp.concatenate(pieces, axis=1).astype(jnp.bfloat16)


def solution(mesh):
    in_specs = (
        P("col", "row"),
        P("row", "col", None),
        P("row", "col", None),
        P("col", "row", None),
        P("row", "col"),
        P("col", "row"),
    )
    out_specs = P("col", "row")
    return jax.shard_map(local, mesh=mesh, in_specs=in_specs, out_specs=out_specs, check_vma=False)
```

```python
import functools

import jax
import jax.numpy as jnp
from jax import lax
from jax.experimental import pallas as pl
from jax.experimental.pallas import tpu as pltpu
from jax.sharding import PartitionSpec as P


def slot_tables(keep, cap):
    rows, cols = keep.shape
    flat = keep.reshape(-1).astype(jnp.int32)
    slot = (jnp.cumsum(flat) - flat).reshape(rows, cols)
    base = jnp.minimum(slot[:, 0], cap - cols)
    index = jnp.where(keep == 1, slot - base[:, None], -1)
    return base.astype(jnp.int32), index.reshape(-1).astype(jnp.int32)


def sparse_kernel(base_ref, index_ref, x_ref, *refs, n_w, group, cols, block):
    w_refs = refs[:n_w * group]
    o_refs = refs[n_w * group:n_w * group + n_w]
    acc_refs = refs[n_w * group + n_w:n_w * group + 2 * n_w]
    panel_refs = refs[n_w * group + 2 * n_w:]
    g = pl.program_id(0)

    @pl.when(g == 0)
    def _():
        for acc in acc_refs:
            acc[...] = jnp.zeros(acc.shape, acc.dtype)

    for rr in range(group):
        for c in range(cols):
            k = index_ref[(g * group + rr) * cols + c]
            for a in range(n_w):
                blk = w_refs[a * group + rr][jnp.maximum(k, 0)]
                panel_refs[a][rr * block:(rr + 1) * block, c * block:(c + 1) * block] = jnp.where(
                    k >= 0, blk, jnp.zeros_like(blk))

    x = x_ref[...]
    for panel, acc in zip(panel_refs, acc_refs):
        acc[...] += jnp.dot(x, panel[...], preferred_element_type=jnp.float32)

    @pl.when(g == pl.num_programs(0) - 1)
    def _():
        for o, acc in zip(o_refs, acc_refs):
            o[...] = acc[...].astype(o.dtype)


def sparse_matmul(x, packed, keep):
    rows, cols = keep.shape
    cap, block, _ = packed[0].shape
    t = x.shape[0]
    n_w = len(packed)
    sizes = (8, 4, 2, 1) if n_w == 1 else (4, 2, 1)
    group = next(s for s in sizes if rows % s == 0)
    base, index = slot_tables(keep, cap)

    def w_spec(rr):
        return pl.BlockSpec(
            (pl.Element(cols), pl.Element(block), pl.Element(block)),
            lambda g, b, i: (b[g * group + rr], 0, 0))

    kernel = functools.partial(sparse_kernel, n_w=n_w, group=group, cols=cols, block=block)
    flops = 2 * t * block * block * rows * cols * n_w
    bytes_accessed = x.size * 2 + n_w * (rows * cols * block * block * 2 + t * cols * block * 2)
    return pl.pallas_call(
        kernel,
        grid_spec=pltpu.PrefetchScalarGridSpec(
            num_scalar_prefetch=2,
            grid=(rows // group,),
            in_specs=[pl.BlockSpec((t, group * block), lambda g, b, i: (0, g))]
            + [w_spec(rr) for _ in range(n_w) for rr in range(group)],
            out_specs=[pl.BlockSpec((t, cols * block), lambda g, b, i: (0, 0))] * n_w,
            scratch_shapes=[pltpu.VMEM((t, cols * block), jnp.float32)] * n_w
            + [pltpu.VMEM((group * block, cols * block), jnp.bfloat16)] * n_w,
        ),
        out_shape=[jax.ShapeDtypeStruct((t, cols * block), jnp.bfloat16)] * n_w,
        compiler_params=pltpu.CompilerParams(dimension_semantics=("arbitrary",)),
        cost_estimate=pl.CostEstimate(flops=flops, transcendentals=0, bytes_accessed=bytes_accessed),
    )(base, index, x, *[p for p in packed for _ in range(group)])


def exchange(x, axis, n, bit):
    pairs = [(i, i ^ (1 << bit)) for i in range(n)]
    return lax.ppermute(x, axis, perm=pairs)


def halving_scatter(streams, axis, n):
    me = lax.axis_index(axis)
    streams = [(list(parts), bits) for parts, bits in streams]
    for step in range(len(streams[0][1])):
        for parts, bits in streams:
            bit = bits[step]
            half = parts[0].shape[0] // 2
            mine = (me >> bit) & 1
            keep = [lax.dynamic_slice_in_dim(p, mine * half, half, axis=0) for p in parts]
            send = [lax.dynamic_slice_in_dim(p, (1 - mine) * half, half, axis=0) for p in parts]
            got = exchange(tuple(s.astype(jnp.bfloat16) for s in send), axis, n, bit)
            parts[:] = [k.astype(jnp.float32) + g.astype(jnp.float32) for k, g in zip(keep, got)]
    return [parts for parts, _ in streams]


def doubling_gather(streams, axis, n):
    me = lax.axis_index(axis)
    xs = [x for x, _ in streams]
    for step in range(len(streams[0][1])):
        for p, (_, bits) in enumerate(streams):
            bit = bits[step]
            got = exchange(xs[p], axis, n, bit)
            low = ((me >> bit) & 1) == 0
            xs[p] = jnp.where(low, jnp.concatenate([xs[p], got], 0), jnp.concatenate([got, xs[p]], 0))
    return xs


def local(tokens, gate_packed, up_packed, down_packed, gate_keep, down_keep):
    n_row = lax.axis_size("row")
    n_col = lax.axis_size("col")
    row_bits = list(range(n_row.bit_length() - 1))
    top = n_col.bit_length() - 1
    col_orders = [list(range(top - 1, -1, -1)), [0] + list(range(top - 1, 0, -1))]
    quarter = tokens.shape[0] // 4
    orders = col_orders * 2
    token_parts = [tokens[q * quarter:(q + 1) * quarter] for q in range(4)]
    segment = jnp.concatenate(doubling_gather(list(zip(token_parts, orders)), "col", n_col), axis=0)
    (gate_rows,) = sparse_matmul(segment, [gate_packed], gate_keep)
    (up_rows,) = sparse_matmul(segment, [up_packed], gate_keep)
    half = gate_rows.shape[0] // 2
    sums = halving_scatter(
        [([gate_rows[:half], up_rows[:half]], row_bits), ([gate_rows[half:], up_rows[half:]], row_bits)],
        "row", n_row)
    hidden_shares = [(jax.nn.silu(g) * u).astype(jnp.bfloat16) for g, u in sums]
    every_hidden = jnp.concatenate(
        doubling_gather([(h, row_bits[::-1]) for h in hidden_shares], "row", n_row), axis=0)
    (partial_out,) = sparse_matmul(every_hidden, [down_packed], down_keep)
    rows_q = partial_out.shape[0] // 4
    out_parts = halving_scatter(
        [([partial_out[q * rows_q:(q + 1) * rows_q]], orders[q][::-1]) for q in range(4)], "col", n_col)
    summed = jnp.concatenate([parts[0] for parts in out_parts], axis=0)
    return summed.astype(jnp.bfloat16)


def solution(mesh):
    in_specs = (
        P("col", "row"),
        P("row", "col", None),
        P("row", "col", None),
        P("col", "row", None),
        P("row", "col"),
        P("col", "row"),
    )
    out_specs = P("col", "row")
    return jax.shard_map(local, mesh=mesh, in_specs=in_specs, out_specs=out_specs, check_vma=False)
```

```python
import functools

import jax
import jax.numpy as jnp
from jax import lax
from jax.experimental import pallas as pl
from jax.experimental.pallas import tpu as pltpu
from jax.sharding import PartitionSpec as P


def slot_tables(keep, cap):
    rows, cols = keep.shape
    flat = keep.reshape(-1).astype(jnp.int32)
    slot = (jnp.cumsum(flat) - flat).reshape(rows, cols)
    base = jnp.minimum(slot[:, 0], cap - cols)
    index = jnp.where(keep == 1, slot - base[:, None], -1)
    return base.astype(jnp.int32), index.reshape(-1).astype(jnp.int32)


def sparse_kernel(base_ref, index_ref, x_ref, *refs, n_w, group, cols, block):
    w_refs = refs[:n_w * group]
    o_refs = refs[n_w * group:n_w * group + n_w]
    acc_refs = refs[n_w * group + n_w:n_w * group + 2 * n_w]
    panel_refs = refs[n_w * group + 2 * n_w:]
    g = pl.program_id(0)

    @pl.when(g == 0)
    def _():
        for acc in acc_refs:
            acc[...] = jnp.zeros(acc.shape, acc.dtype)

    for rr in range(group):
        for c in range(cols):
            k = index_ref[(g * group + rr) * cols + c]
            for a in range(n_w):
                blk = w_refs[a * group + rr][jnp.maximum(k, 0)]
                panel_refs[a][rr * block:(rr + 1) * block, c * block:(c + 1) * block] = jnp.where(
                    k >= 0, blk, jnp.zeros_like(blk))

    x = x_ref[...]
    for panel, acc in zip(panel_refs, acc_refs):
        acc[...] += jnp.dot(x, panel[...], preferred_element_type=jnp.float32)

    @pl.when(g == pl.num_programs(0) - 1)
    def _():
        for o, acc in zip(o_refs, acc_refs):
            o[...] = acc[...].astype(o.dtype)


def sparse_matmul(x, packed, keep):
    rows, cols = keep.shape
    cap, block, _ = packed[0].shape
    t = x.shape[0]
    n_w = len(packed)
    group = next(s for s in (4, 2, 1) if rows % s == 0)
    base, index = slot_tables(keep, cap)

    def w_spec(rr):
        return pl.BlockSpec(
            (pl.Element(cols), pl.Element(block), pl.Element(block)),
            lambda g, b, i: (b[g * group + rr], 0, 0))

    kernel = functools.partial(sparse_kernel, n_w=n_w, group=group, cols=cols, block=block)
    flops = 2 * t * block * block * rows * cols * n_w
    bytes_accessed = x.size * 2 + n_w * (rows * cols * block * block * 2 + t * cols * block * 2)
    return pl.pallas_call(
        kernel,
        grid_spec=pltpu.PrefetchScalarGridSpec(
            num_scalar_prefetch=2,
            grid=(rows // group,),
            in_specs=[pl.BlockSpec((t, group * block), lambda g, b, i: (0, g))]
            + [w_spec(rr) for _ in range(n_w) for rr in range(group)],
            out_specs=[pl.BlockSpec((t, cols * block), lambda g, b, i: (0, 0))] * n_w,
            scratch_shapes=[pltpu.VMEM((t, cols * block), jnp.float32)] * n_w
            + [pltpu.VMEM((group * block, cols * block), jnp.bfloat16)] * n_w,
        ),
        out_shape=[jax.ShapeDtypeStruct((t, cols * block), jnp.bfloat16)] * n_w,
        compiler_params=pltpu.CompilerParams(dimension_semantics=("arbitrary",)),
        cost_estimate=pl.CostEstimate(flops=flops, transcendentals=0, bytes_accessed=bytes_accessed),
    )(base, index, x, *[p for p in packed for _ in range(group)])


def exchange(x, axis, n, bit):
    pairs = [(i, i ^ (1 << bit)) for i in range(n)]
    return lax.ppermute(x, axis, perm=pairs)


def halving_scatter(streams, axis, n):
    me = lax.axis_index(axis)
    streams = [(list(parts), bits) for parts, bits in streams]
    for step in range(len(streams[0][1])):
        for parts, bits in streams:
            bit = bits[step]
            half = parts[0].shape[0] // 2
            mine = (me >> bit) & 1
            keep = [lax.dynamic_slice_in_dim(p, mine * half, half, axis=0) for p in parts]
            send = [lax.dynamic_slice_in_dim(p, (1 - mine) * half, half, axis=0) for p in parts]
            got = exchange(tuple(s.astype(jnp.bfloat16) for s in send), axis, n, bit)
            parts[:] = [k.astype(jnp.float32) + g.astype(jnp.float32) for k, g in zip(keep, got)]
    return [parts for parts, _ in streams]


def doubling_gather(streams, axis, n):
    me = lax.axis_index(axis)
    xs = [x for x, _ in streams]
    for step in range(len(streams[0][1])):
        for p, (_, bits) in enumerate(streams):
            bit = bits[step]
            got = exchange(xs[p], axis, n, bit)
            low = ((me >> bit) & 1) == 0
            xs[p] = jnp.where(low, jnp.concatenate([xs[p], got], 0), jnp.concatenate([got, xs[p]], 0))
    return xs


def local(tokens, gate_packed, up_packed, down_packed, gate_keep, down_keep):
    n_row = lax.axis_size("row")
    n_col = lax.axis_size("col")
    row_bits = list(range(n_row.bit_length() - 1))
    top = n_col.bit_length() - 1
    col_orders = [list(range(top - 1, -1, -1)), [top - 1, 0] + list(range(top - 2, 0, -1))]
    quarter = tokens.shape[0] // 4
    orders = col_orders * 2
    token_parts = [tokens[q * quarter:(q + 1) * quarter] for q in range(4)]
    segment = jnp.concatenate(doubling_gather(list(zip(token_parts, orders)), "col", n_col), axis=0)
    gate_rows, up_rows = sparse_matmul(segment, [gate_packed, up_packed], gate_keep)
    half = gate_rows.shape[0] // 2
    sums = halving_scatter(
        [([gate_rows[:half], up_rows[:half]], row_bits), ([gate_rows[half:], up_rows[half:]], row_bits)],
        "row", n_row)
    hidden_shares = [(jax.nn.silu(g) * u).astype(jnp.bfloat16) for g, u in sums]
    every_hidden = jnp.concatenate(
        doubling_gather([(h, row_bits[::-1]) for h in hidden_shares], "row", n_row), axis=0)
    (partial_out,) = sparse_matmul(every_hidden, [down_packed], down_keep)
    rows_q = partial_out.shape[0] // 4
    out_parts = halving_scatter(
        [([partial_out[q * rows_q:(q + 1) * rows_q]], orders[q][::-1]) for q in range(4)], "col", n_col)
    summed = jnp.concatenate([parts[0] for parts in out_parts], axis=0)
    return summed.astype(jnp.bfloat16)


def solution(mesh):
    in_specs = (
        P("col", "row"),
        P("row", "col", None),
        P("row", "col", None),
        P("col", "row", None),
        P("row", "col"),
        P("col", "row"),
    )
    out_specs = P("col", "row")
    return jax.shard_map(local, mesh=mesh, in_specs=in_specs, out_specs=out_specs, check_vma=False)
```

```python
import functools

import jax
import jax.numpy as jnp
from jax import lax
from jax.experimental import pallas as pl
from jax.experimental.pallas import tpu as pltpu
from jax.sharding import PartitionSpec as P


def slot_tables(keep, cap):
    rows, cols = keep.shape
    flat = keep.reshape(-1).astype(jnp.int32)
    slot = (jnp.cumsum(flat) - flat).reshape(rows, cols)
    base = jnp.minimum(slot[:, 0], cap - cols)
    index = jnp.where(keep == 1, slot - base[:, None], -1)
    return base.astype(jnp.int32), index.reshape(-1).astype(jnp.int32)


def sparse_kernel(base_ref, index_ref, x_ref, *refs, n_w, group, cols, block):
    w_refs = refs[:n_w * group]
    o_refs = refs[n_w * group:n_w * group + n_w]
    acc_refs = refs[n_w * group + n_w:n_w * group + 2 * n_w]
    panel_refs = refs[n_w * group + 2 * n_w:]
    g = pl.program_id(0)

    @pl.when(g == 0)
    def _():
        for acc in acc_refs:
            acc[...] = jnp.zeros(acc.shape, acc.dtype)

    for rr in range(group):
        for c in range(cols):
            k = index_ref[(g * group + rr) * cols + c]
            for a in range(n_w):
                blk = w_refs[a * group + rr][jnp.maximum(k, 0)]
                panel_refs[a][rr * block:(rr + 1) * block, c * block:(c + 1) * block] = jnp.where(
                    k >= 0, blk, jnp.zeros_like(blk))

    x = x_ref[...]
    for panel, acc in zip(panel_refs, acc_refs):
        acc[...] += jnp.dot(x, panel[...], preferred_element_type=jnp.float32)

    @pl.when(g == pl.num_programs(0) - 1)
    def _():
        for o, acc in zip(o_refs, acc_refs):
            o[...] = acc[...].astype(o.dtype)


def sparse_matmul(x, packed, keep):
    rows, cols = keep.shape
    cap, block, _ = packed[0].shape
    t = x.shape[0]
    n_w = len(packed)
    group = next(s for s in (4, 2, 1) if rows % s == 0)
    base, index = slot_tables(keep, cap)

    def w_spec(rr):
        return pl.BlockSpec(
            (pl.Element(cols), pl.Element(block), pl.Element(block)),
            lambda g, b, i: (b[g * group + rr], 0, 0))

    kernel = functools.partial(sparse_kernel, n_w=n_w, group=group, cols=cols, block=block)
    flops = 2 * t * block * block * rows * cols * n_w
    bytes_accessed = x.size * 2 + n_w * (rows * cols * block * block * 2 + t * cols * block * 2)
    return pl.pallas_call(
        kernel,
        grid_spec=pltpu.PrefetchScalarGridSpec(
            num_scalar_prefetch=2,
            grid=(rows // group,),
            in_specs=[pl.BlockSpec((t, group * block), lambda g, b, i: (0, g))]
            + [w_spec(rr) for _ in range(n_w) for rr in range(group)],
            out_specs=[pl.BlockSpec((t, cols * block), lambda g, b, i: (0, 0))] * n_w,
            scratch_shapes=[pltpu.VMEM((t, cols * block), jnp.float32)] * n_w
            + [pltpu.VMEM((group * block, cols * block), jnp.bfloat16)] * n_w,
        ),
        out_shape=[jax.ShapeDtypeStruct((t, cols * block), jnp.bfloat16)] * n_w,
        compiler_params=pltpu.CompilerParams(dimension_semantics=("arbitrary",)),
        cost_estimate=pl.CostEstimate(flops=flops, transcendentals=0, bytes_accessed=bytes_accessed),
    )(base, index, x, *[p for p in packed for _ in range(group)])


def exchange(x, axis, n, bit):
    pairs = [(i, i ^ (1 << bit)) for i in range(n)]
    return lax.ppermute(x, axis, perm=pairs)


def halving_scatter(streams, axis, n):
    me = lax.axis_index(axis)
    streams = [(list(parts), bits) for parts, bits in streams]
    for step in range(len(streams[0][1])):
        for parts, bits in streams:
            bit = bits[step]
            half = parts[0].shape[0] // 2
            mine = (me >> bit) & 1
            keep = [lax.dynamic_slice_in_dim(p, mine * half, half, axis=0) for p in parts]
            send = [lax.dynamic_slice_in_dim(p, (1 - mine) * half, half, axis=0) for p in parts]
            got = exchange(tuple(s.astype(jnp.bfloat16) for s in send), axis, n, bit)
            parts[:] = [k.astype(jnp.float32) + g.astype(jnp.float32) for k, g in zip(keep, got)]
    return [parts for parts, _ in streams]


def doubling_gather(streams, axis, n):
    me = lax.axis_index(axis)
    xs = [x for x, _ in streams]
    for step in range(len(streams[0][1])):
        for p, (_, bits) in enumerate(streams):
            bit = bits[step]
            got = exchange(xs[p], axis, n, bit)
            low = ((me >> bit) & 1) == 0
            xs[p] = jnp.where(low, jnp.concatenate([xs[p], got], 0), jnp.concatenate([got, xs[p]], 0))
    return xs


def local(tokens, gate_packed, up_packed, down_packed, gate_keep, down_keep):
    n_row = lax.axis_size("row")
    n_col = lax.axis_size("col")
    row_bits = list(range(n_row.bit_length() - 1))
    top = n_col.bit_length() - 1
    col_orders = [list(range(top - 1, -1, -1)), [top - 1, 0] + list(range(top - 2, 0, -1))]
    quarter = tokens.shape[0] // 4
    orders = [col_orders[0]] * 3 + [col_orders[1]]
    token_parts = [tokens[q * quarter:(q + 1) * quarter] for q in range(4)]
    segment = jnp.concatenate(doubling_gather(list(zip(token_parts, orders)), "col", n_col), axis=0)
    gate_rows, up_rows = sparse_matmul(segment, [gate_packed, up_packed], gate_keep)
    half = gate_rows.shape[0] // 2
    sums = halving_scatter(
        [([gate_rows[:half], up_rows[:half]], row_bits), ([gate_rows[half:], up_rows[half:]], row_bits)],
        "row", n_row)
    hidden_shares = [(jax.nn.silu(g) * u).astype(jnp.bfloat16) for g, u in sums]
    every_hidden = jnp.concatenate(
        doubling_gather([(h, row_bits[::-1]) for h in hidden_shares], "row", n_row), axis=0)
    (partial_out,) = sparse_matmul(every_hidden, [down_packed], down_keep)
    rows_q = partial_out.shape[0] // 4
    out_parts = halving_scatter(
        [([partial_out[q * rows_q:(q + 1) * rows_q]], orders[q][::-1]) for q in range(4)], "col", n_col)
    summed = jnp.concatenate([parts[0] for parts in out_parts], axis=0)
    return summed.astype(jnp.bfloat16)


def solution(mesh):
    in_specs = (
        P("col", "row"),
        P("row", "col", None),
        P("row", "col", None),
        P("col", "row", None),
        P("row", "col"),
        P("col", "row"),
    )
    out_specs = P("col", "row")
    return jax.shard_map(local, mesh=mesh, in_specs=in_specs, out_specs=out_specs, check_vma=False)
```

```python
import functools

import jax
import jax.numpy as jnp
from jax import lax
from jax.experimental import pallas as pl
from jax.experimental.pallas import tpu as pltpu
from jax.sharding import PartitionSpec as P


def slot_tables(keep, cap):
    rows, cols = keep.shape
    flat = keep.reshape(-1).astype(jnp.int32)
    slot = (jnp.cumsum(flat) - flat).reshape(rows, cols)
    base = jnp.minimum(slot[:, 0], cap - cols)
    index = jnp.where(keep == 1, slot - base[:, None], -1)
    return base.astype(jnp.int32), index.reshape(-1).astype(jnp.int32)


def sparse_kernel(base_ref, index_ref, x_ref, *refs, n_w, group, cols, block):
    w_refs = refs[:n_w * group]
    o_refs = refs[n_w * group:n_w * group + n_w]
    acc_refs = refs[n_w * group + n_w:n_w * group + 2 * n_w]
    panel_refs = refs[n_w * group + 2 * n_w:]
    g = pl.program_id(0)

    @pl.when(g == 0)
    def _():
        for acc in acc_refs:
            acc[...] = jnp.zeros(acc.shape, acc.dtype)

    for rr in range(group):
        for c in range(cols):
            k = index_ref[(g * group + rr) * cols + c]
            for a in range(n_w):
                blk = w_refs[a * group + rr][jnp.maximum(k, 0)]
                panel_refs[a][rr * block:(rr + 1) * block, c * block:(c + 1) * block] = jnp.where(
                    k >= 0, blk, jnp.zeros_like(blk))

    x = x_ref[...]
    for panel, acc in zip(panel_refs, acc_refs):
        acc[...] += jnp.dot(x, panel[...], preferred_element_type=jnp.float32)

    @pl.when(g == pl.num_programs(0) - 1)
    def _():
        for o, acc in zip(o_refs, acc_refs):
            o[...] = acc[...].astype(o.dtype)


def sparse_matmul(x, packed, keep):
    rows, cols = keep.shape
    cap, block, _ = packed[0].shape
    t = x.shape[0]
    n_w = len(packed)
    group = next(s for s in (4, 2, 1) if rows % s == 0)
    base, index = slot_tables(keep, cap)

    def w_spec(rr):
        return pl.BlockSpec(
            (pl.Element(cols), pl.Element(block), pl.Element(block)),
            lambda g, b, i: (b[g * group + rr], 0, 0))

    kernel = functools.partial(sparse_kernel, n_w=n_w, group=group, cols=cols, block=block)
    flops = 2 * t * block * block * rows * cols * n_w
    bytes_accessed = x.size * 2 + n_w * (rows * cols * block * block * 2 + t * cols * block * 2)
    return pl.pallas_call(
        kernel,
        grid_spec=pltpu.PrefetchScalarGridSpec(
            num_scalar_prefetch=2,
            grid=(rows // group,),
            in_specs=[pl.BlockSpec((t, group * block), lambda g, b, i: (0, g))]
            + [w_spec(rr) for _ in range(n_w) for rr in range(group)],
            out_specs=[pl.BlockSpec((t, cols * block), lambda g, b, i: (0, 0))] * n_w,
            scratch_shapes=[pltpu.VMEM((t, cols * block), jnp.float32)] * n_w
            + [pltpu.VMEM((group * block, cols * block), jnp.bfloat16)] * n_w,
        ),
        out_shape=[jax.ShapeDtypeStruct((t, cols * block), jnp.bfloat16)] * n_w,
        compiler_params=pltpu.CompilerParams(dimension_semantics=("arbitrary",)),
        cost_estimate=pl.CostEstimate(flops=flops, transcendentals=0, bytes_accessed=bytes_accessed),
    )(base, index, x, *[p for p in packed for _ in range(group)])


def exchange(x, axis, n, bit):
    pairs = [(i, i ^ (1 << bit)) for i in range(n)]
    return lax.ppermute(x, axis, perm=pairs)


def halving_scatter(streams, axis, n):
    me = lax.axis_index(axis)
    streams = [(list(parts), bits) for parts, bits in streams]
    for step in range(len(streams[0][1])):
        for parts, bits in streams:
            bit = bits[step]
            half = parts[0].shape[0] // 2
            mine = (me >> bit) & 1
            keep = [lax.dynamic_slice_in_dim(p, mine * half, half, axis=0) for p in parts]
            send = [lax.dynamic_slice_in_dim(p, (1 - mine) * half, half, axis=0) for p in parts]
            got = exchange(tuple(s.astype(jnp.bfloat16) for s in send), axis, n, bit)
            parts[:] = [k.astype(jnp.float32) + g.astype(jnp.float32) for k, g in zip(keep, got)]
    return [parts for parts, _ in streams]


def doubling_gather(streams, axis, n):
    me = lax.axis_index(axis)
    xs = [x for x, _ in streams]
    for step in range(len(streams[0][1])):
        for p, (_, bits) in enumerate(streams):
            bit = bits[step]
            got = exchange(xs[p], axis, n, bit)
            low = ((me >> bit) & 1) == 0
            xs[p] = jnp.where(low, jnp.concatenate([xs[p], got], 0), jnp.concatenate([got, xs[p]], 0))
    return xs


def local(tokens, gate_packed, up_packed, down_packed, gate_keep, down_keep):
    n_row = lax.axis_size("row")
    n_col = lax.axis_size("col")
    row_bits = list(range(n_row.bit_length() - 1))
    top = n_col.bit_length() - 1
    col_orders = [list(range(top - 1, -1, -1)), [top - 1, 0] + list(range(top - 2, 0, -1))]
    quarter = tokens.shape[0] // 4
    rest = list(range(2, top))
    orders = [[1, 0] + rest, [1] + rest + [0], col_orders[1], col_orders[0]]
    token_parts = [tokens[q * quarter:(q + 1) * quarter] for q in range(4)]
    segment = jnp.concatenate(doubling_gather(list(zip(token_parts, orders)), "col", n_col), axis=0)
    gate_rows, up_rows = sparse_matmul(segment, [gate_packed, up_packed], gate_keep)
    half = gate_rows.shape[0] // 2
    sums = halving_scatter(
        [([gate_rows[:half], up_rows[:half]], row_bits), ([gate_rows[half:], up_rows[half:]], row_bits)],
        "row", n_row)
    hidden_shares = [(jax.nn.silu(g) * u).astype(jnp.bfloat16) for g, u in sums]
    every_hidden = jnp.concatenate(
        doubling_gather([(h, row_bits[::-1]) for h in hidden_shares], "row", n_row), axis=0)
    (partial_out,) = sparse_matmul(every_hidden, [down_packed], down_keep)
    rows_q = partial_out.shape[0] // 4
    out_parts = halving_scatter(
        [([partial_out[q * rows_q:(q + 1) * rows_q]], orders[q][::-1]) for q in range(4)], "col", n_col)
    summed = jnp.concatenate([parts[0] for parts in out_parts], axis=0)
    return summed.astype(jnp.bfloat16)


def solution(mesh):
    in_specs = (
        P("col", "row"),
        P("row", "col", None),
        P("row", "col", None),
        P("col", "row", None),
        P("row", "col"),
        P("col", "row"),
    )
    out_specs = P("col", "row")
    return jax.shard_map(local, mesh=mesh, in_specs=in_specs, out_specs=out_specs, check_vma=False)
```
